32 devices in a mesh: feat: 8 (over y, x, core), tok: 4 (over z).
Axes of the slice: x: 2, y: 2, z: 4, core: 2. Of those that a mesh axis runs over, the one named last changes fastest.
Arguments:
- residual: bfloat16 [256, 4608], P('tok', 'feat'), may hold values from -700 to 700
- enc_weight: bfloat16 [4608, 8192], P(None, ('feat', 'tok')), may hold values from -0.09375 to 0.09375
- enc_bias: float32 [8192], P(('feat', 'tok')), may hold values from -3 to 3
- threshold: float32 [8192], P(('feat', 'tok')), may hold values from 0.25 to 2.5
- probe_weight: bfloat16 [8192, 16], P(('feat', 'tok')), may hold values from -0.375 to 0.375
- probe_bias: float32 [16], replicated, may hold values from -3 to 3
- labels: int32 [256], replicated, may hold values from 0 to 15
Outputs:
- probe_grad: float32 [8192, 16], P(('feat', 'tok'))
- token_loss: float32 [256], P(('feat', 'tok'))
The draws below stay inside these ranges and needn't reach their ends.
All inputs are finite; a program needn't handle non-finite values.
Results may differ from the reference program's by a relative error of at most 0.0034.
Values may be sent and summed in bfloat16 or wider, within the bound.
No kernel may reach another device: no remote copies, remote signals or barrier semaphores. Data moves between devices by JAX's collectives and lax.ppermute only.
A program may use at most 64 MiB of HBM per device.

```python
import math
import jax
import jax.numpy as jnp
from jax import lax

D = 4608
FEAT_DEV = 256
CLASSES = 16
TOKENS = 256
FEATURES = 8192
N_TOK = 4


def draw_residual(key, part):
    key_base, key_cols, key_rows = jax.random.split(jax.random.fold_in(key, 11), 3)
    ramp = jnp.arange(D, dtype=jnp.float32) / max(D - 1, 1)
    col_spread = jnp.power(10.0, jax.random.uniform(key_cols, (D,), jnp.float32))
    row_spread = jnp.power(10.0, jax.random.uniform(key_rows, (TOKENS, 1), jnp.float32))
    base = jnp.clip(jax.random.normal(key_base, (TOKENS, D), jnp.float32), -4.0, 4.0)
    col_scale = col_spread * jnp.power(3.0, 0.5 * ramp)
    return (base * row_spread * col_scale[None, :]).astype(jnp.bfloat16)


def place_ends(drawn, own_key, smallest, largest):
    longest = drawn.shape.index(max(drawn.shape))
    spots = []
    for shift in (0, 1):
        where = [jax.random.randint(jax.random.fold_in(own_key, axis), (), 0, length) for axis, length in enumerate(drawn.shape)]
        where[longest] = (where[longest] + shift) % drawn.shape[longest]
        spots.append(tuple(where))
    return drawn.at[spots[0]].set(smallest).at[spots[1]].set(largest)


def level_of(stream_key, shape, pieces, least, top_value):
    factor_of, own = 1.0, jax.random.fold_in(stream_key, 6)
    for axis_at, parts in pieces:
        draws = jnp.exp(jax.random.uniform(jax.random.fold_in(own, axis_at), (parts,), jnp.float32, least / len(pieces), top_value / len(pieces)))
        factor_of = factor_of * jnp.repeat(draws, shape[axis_at] // parts).reshape([-1 if axis == axis_at else 1 for axis in range(len(shape))])
    return factor_of


def normal_values(own_key, shape, spread, reach, shards=(), kind=jnp.bfloat16):
    array = jax.random.normal(own_key, shape, jnp.float32) * spread
    if len(shards) > 0:
        array = level_of(own_key, shape, shards, -0.22, 0.18) * array
    return jnp.clip(array, min=-reach, max=reach).astype(kind)


def setup_inputs(seed: int = 0) -> dict:
    keys = jax.random.split(jax.random.key(seed), 8)
    residual = draw_residual(jax.random.fold_in(keys[7], 71), 0)
    enc_weight = normal_values(keys[1], (D, FEATURES), D ** -0.5, 0.09375, ((1, 32),))
    enc_bias = normal_values(keys[2], (FEATURES,), 0.5, 3.0, ((0, 32),), jnp.float32)
    threshold = jnp.clip(jnp.exp(math.log(2.5) - 2.3025851 * jax.random.uniform(keys[3], (FEATURES,), jnp.float32) ** level_of(keys[3], (FEATURES,), ((0, 32),), -0.2, 0.2)), 0.25, 2.5)
    probe_weight = normal_values(keys[4], (FEATURES, CLASSES), (FEATURES // 32) ** -0.5, 0.375, ((0, 32),))
    probe_bias = normal_values(keys[5], (CLASSES,), 1.0, 3.0, (), jnp.float32)
    labels = place_ends(jax.random.randint(keys[6], (TOKENS,), 0, CLASSES), jax.random.fold_in(keys[6], 1), 0, CLASSES - 1).astype(jnp.int32)
    return dict(residual=residual, enc_weight=enc_weight, enc_bias=enc_bias, threshold=threshold, probe_weight=probe_weight, probe_bias=probe_bias, labels=labels)


epsilon = 1e-06
smooth_width = 0.125

def reference(residual, enc_weight, enc_bias, threshold, probe_weight, probe_bias, labels):
    values = residual.astype(jnp.float32)
    mean_square = lax.optimization_barrier(jnp.mean(values * values, axis=1, keepdims=True))
    normed = (values * lax.rsqrt(mean_square + epsilon)).astype(jnp.bfloat16)
    count = FEATURES // (FEAT_DEV * N_TOK)
    width_block = FEAT_DEV * N_TOK
    weight_blocks = enc_weight.reshape(D, count, width_block).transpose(1, 0, 2)
    bias_blocks = enc_bias.reshape(count, width_block)
    thresh_blocks = threshold.reshape(count, width_block)
    probe_blocks = probe_weight.reshape(count, width_block, CLASSES)

    def encode_block(total, block):
        weight_part, bias_part, thresh_part, probe_part = block
        preact = jnp.dot(normed, weight_part, preferred_element_type=jnp.float32) + bias_part
        features = (preact * jax.nn.sigmoid((preact - thresh_part) / smooth_width)).astype(jnp.bfloat16)
        total = total + jnp.dot(features, probe_part, preferred_element_type=jnp.float32)
        return (total, features)
    zeros_init = jnp.zeros((TOKENS, CLASSES), jnp.float32)
    logits, feature_blocks = lax.scan(encode_block, zeros_init, (weight_blocks, bias_blocks, thresh_blocks, probe_blocks))
    logits = logits + probe_bias
    exps = jnp.exp(logits)
    totals = lax.optimization_barrier(jnp.sum(exps, axis=1, keepdims=True))
    onehot = (labels[:, None] == jnp.arange(CLASSES, dtype=jnp.int32)[None, :]).astype(jnp.float32)
    token_loss = jnp.log(totals[:, 0]) - lax.optimization_barrier(jnp.sum(onehot * logits, axis=1))
    delta = (exps / totals - onehot).astype(jnp.bfloat16)

    def grad_block(features):
        return jnp.dot(features.T, delta, preferred_element_type=jnp.float32)
    probe_grad = lax.map(grad_block, feature_blocks).reshape(FEATURES, CLASSES)
    return (probe_grad, token_loss)
```

```python
import jax
import jax.numpy as jnp
from jax import lax
from jax.sharding import PartitionSpec as P

epsilon = 1e-06
smooth_width = 0.125


def bits_of(n):
    count = n.bit_length() - 1
    assert 1 << count == n
    return count


def exchange(value, axis, bit):
    size = lax.axis_size(axis)
    return lax.ppermute(value, axis, [(i, i ^ (1 << bit)) for i in range(size)])


def gather_steps():
    tok_bits = bits_of(lax.axis_size("tok"))
    feat_bits = bits_of(lax.axis_size("feat"))
    steps = [("tok", b) for b in reversed(range(tok_bits))]
    steps += [("feat", b) for b in range(1, feat_bits)] + [("feat", 0)]
    return steps


def gather_all(block, steps):
    rows, cols = block.shape
    held = block
    done = {"tok": [], "feat": []}
    for axis, bit in steps:
        other = exchange(held, axis, bit)
        mine = (lax.axis_index(axis) >> bit) & 1
        low = jnp.where(mine == 0, held, other)
        high = jnp.where(mine == 0, other, held)
        above = sum(1 for b in done[axis] if b > bit)
        start = 0 if axis == "tok" else len(done["tok"]) + 1
        held = jnp.stack([low, high], axis=start + above)
        done[axis].append(bit)
    return held, len(done["tok"])


def reduce_all(value, steps):
    for axis, bit in steps:
        value = value + exchange(value, axis, bit)
    return value


def local(residual, enc_weight, enc_bias, threshold, probe_weight, probe_bias, labels):
    steps = gather_steps()
    held, tok_dims = gather_all(residual, steps)
    held = lax.optimization_barrier(held)
    values = held.astype(jnp.float32)
    width_axes = tuple(range(tok_dims + 1, held.ndim))
    full_width = residual.shape[1] * lax.axis_size("feat")
    mean_square = jnp.sum(values * values, axis=width_axes, keepdims=True) / full_width
    normed = (values * lax.rsqrt(mean_square + epsilon)).astype(jnp.bfloat16)
    normed = normed.reshape(residual.shape[0] * lax.axis_size("tok"), full_width)
    preact = jnp.dot(normed, enc_weight, preferred_element_type=jnp.float32)
    encode_preact = preact + enc_bias
    features = (encode_preact * jax.nn.sigmoid((encode_preact - threshold) / smooth_width)).astype(
        jnp.bfloat16
    )
    partial_value = jnp.dot(features, probe_weight, preferred_element_type=jnp.float32)
    num_tokens = features.shape[0]
    share_rows = num_tokens // lax.axis_size(("feat", "tok"))
    position = lax.axis_index(("feat", "tok"))
    class_ids = jnp.arange(probe_weight.shape[1], dtype=jnp.int32)
    logits = reduce_all(partial_value, steps)
    softmax_logits = logits + probe_bias
    exps = jnp.exp(softmax_logits)
    totals = jnp.sum(exps, axis=1, keepdims=True)
    onehot = (labels[:, None] == class_ids[None, :]).astype(jnp.float32)
    losses = jnp.log(totals[:, 0]) - jnp.sum(onehot * softmax_logits, axis=1)
    delta = (exps / totals - onehot).astype(jnp.bfloat16)
    token_loss = lax.dynamic_slice_in_dim(losses, position * share_rows, share_rows, 0)
    gradient = jnp.dot(features.T, delta, preferred_element_type=jnp.float32)
    return (gradient, token_loss)


def solution(mesh):
    in_specs = (
        P("tok", "feat"),
        P(None, ("feat", "tok")),
        P(("feat", "tok")),
        P(("feat", "tok")),
        P(("feat", "tok"), None),
        P(),
        P(),
    )
    out_specs = (P(("feat", "tok"), None), P(("feat", "tok")))
    return jax.shard_map(local, mesh=mesh, in_specs=in_specs, out_specs=out_specs, check_vma=False)
```

```python
import jax
import jax.numpy as jnp
from jax import lax
from jax.sharding import PartitionSpec as P

epsilon = 1e-06
smooth_width = 0.125


def bits_of(n):
    count = n.bit_length() - 1
    assert 1 << count == n
    return count


def exchange(value, axis, offset):
    size = lax.axis_size(axis)
    return lax.ppermute(value, axis, [(i, i ^ offset) for i in range(size)])


def phases():
    tok = lax.axis_size("tok")
    feat = lax.axis_size("feat")
    return [
        ("tok", list(range(1, tok))),
        ("feat", list(range(2, feat, 2))),
        ("feat", [1]),
    ]


def gather_blocks(block):
    held = block[None]
    offsets = {"tok": [0], "feat": [0]}
    for axis, partners in phases():
        pieces = [held] + [exchange(held, axis, k) for k in partners]
        held = jnp.concatenate(pieces, axis=1 if axis == "tok" else 0)
        offsets[axis] = [k ^ old for k in [0] + partners for old in offsets[axis]]
    return held, offsets


def inverse(offsets):
    where = [0] * len(offsets)
    for p, k in enumerate(offsets):
        where[k] = p
    return jnp.array(where, jnp.int32)


def reduce_sum(value):
    for axis, partners in phases():
        ks = [0] + partners
        pieces = jnp.stack([value] + [exchange(value, axis, k) for k in partners])
        mine = lax.axis_index(axis)
        order = [k for k in sorted(ks)]
        sources = [mine ^ k for k in ks]
        rank = jnp.stack(sources)
        pieces = pieces[jnp.argsort(rank)]
        total = pieces[0]
        for i in range(1, len(ks)):
            total = total + pieces[i]
        value = total
    return value


def local(residual, enc_weight, enc_bias, threshold, probe_weight, probe_bias, labels):
    rows, cols = residual.shape
    my_tok = lax.axis_index("tok")
    my_feat = lax.axis_index("feat")
    held, offsets = gather_blocks(residual)
    held = lax.optimization_barrier(held)
    values = held.astype(jnp.float32)
    full_width = cols * lax.axis_size("feat")
    mean_square = jnp.sum(values * values, axis=(0, 2), keepdims=True) / full_width
    normed = (values * lax.rsqrt(mean_square + epsilon)).astype(jnp.bfloat16)
    feat_ids = my_feat ^ jnp.array(offsets["feat"], jnp.int32)
    weight_blocks = jnp.take(enc_weight.reshape(-1, cols, enc_weight.shape[1]), feat_ids, axis=0)
    preact = lax.dot_general(
        normed, weight_blocks, (((0, 2), (0, 1)), ((), ())), preferred_element_type=jnp.float32
    )
    encode_preact = preact + enc_bias
    features = (encode_preact * jax.nn.sigmoid((encode_preact - threshold) / smooth_width)).astype(
        jnp.bfloat16
    )
    partial_value = jnp.dot(features, probe_weight, preferred_element_type=jnp.float32)
    classes = probe_weight.shape[1]
    tok_count = len(offsets["tok"])
    positions = inverse(offsets["tok"])[jnp.arange(tok_count, dtype=jnp.int32) ^ my_tok]
    partial_value = jnp.take(partial_value.reshape(tok_count, rows, classes), positions, axis=0)
    partial_value = partial_value.reshape(tok_count * rows, classes)
    num_tokens = tok_count * rows
    share_rows = num_tokens // lax.axis_size(("feat", "tok"))
    position = lax.axis_index(("feat", "tok"))
    class_ids = jnp.arange(classes, dtype=jnp.int32)
    logits = reduce_sum(partial_value)
    softmax_logits = logits + probe_bias
    exps = jnp.exp(softmax_logits)
    totals = jnp.sum(exps, axis=1, keepdims=True)
    onehot = (labels[:, None] == class_ids[None, :]).astype(jnp.float32)
    losses = jnp.log(totals[:, 0]) - jnp.sum(onehot * softmax_logits, axis=1)
    delta = (exps / totals - onehot).astype(jnp.bfloat16)
    token_loss = lax.dynamic_slice_in_dim(losses, position * share_rows, share_rows, 0)
    token_ids = my_tok ^ jnp.array(offsets["tok"], jnp.int32)
    delta_held = jnp.take(delta.reshape(tok_count, rows, classes), token_ids, axis=0)
    delta_held = delta_held.reshape(num_tokens, classes)
    gradient = jnp.dot(features.T, delta_held, preferred_element_type=jnp.float32)
    return (gradient, token_loss)


def solution(mesh):
    in_specs = (
        P("tok", "feat"),
        P(None, ("feat", "tok")),
        P(("feat", "tok")),
        P(("feat", "tok")),
        P(("feat", "tok"), None),
        P(),
        P(),
    )
    out_specs = (P(("feat", "tok"), None), P(("feat", "tok")))
    return jax.shard_map(local, mesh=mesh, in_specs=in_specs, out_specs=out_specs, check_vma=False)
```

```python
import jax
import jax.numpy as jnp
from jax import lax
from jax.sharding import PartitionSpec as P

epsilon = 1e-06
smooth_width = 0.125


def exchange(value, axis, offset):
    size = lax.axis_size(axis)
    return lax.ppermute(value, axis, [(i, i ^ offset) for i in range(size)])


def tok_partners():
    return list(range(1, lax.axis_size("tok")))


def chip_partners():
    return list(range(2, lax.axis_size("feat"), 2))


def gather_pieces(block):
    rows, cols = block.shape
    my_tok = lax.axis_index("tok")
    my_feat = lax.axis_index("feat")
    column = jnp.zeros((rows * lax.axis_size("tok"), cols), block.dtype)
    column = lax.dynamic_update_slice(column, block, (my_tok * rows, 0))
    for k in tok_partners():
        got = exchange(block, "tok", k)
        column = lax.dynamic_update_slice(column, got, ((my_tok ^ k) * rows, 0))
    mine = [(my_feat, column)]
    for k in chip_partners():
        mine.append((my_feat ^ k, exchange(column, "feat", k)))
    bundle = exchange(jnp.stack([piece for _, piece in mine]), "feat", 1)
    pieces = list(mine)
    for j, k in enumerate([0] + chip_partners()):
        pieces.append((my_feat ^ 1 ^ k, bundle[j]))
    return pieces


def reduce_sum(value):
    total = value
    for k in tok_partners():
        total = total + exchange(value, "tok", k)
    value = total
    total = value
    for k in chip_partners():
        total = total + exchange(value, "feat", k)
    value = total
    return value + exchange(value, "feat", 1)


def local(residual, enc_weight, enc_bias, threshold, probe_weight, probe_bias, labels):
    rows, cols = residual.shape
    pieces = gather_pieces(residual)
    full_width = cols * lax.axis_size("feat")
    square_sum = None
    for _, piece in pieces:
        values = piece.astype(jnp.float32)
        part = jnp.sum(values * values, axis=1)
        square_sum = part if square_sum is None else square_sum + part
    scale = lax.rsqrt(square_sum / full_width + epsilon)[:, None]
    preact = None
    for feat_id, piece in pieces:
        normed = (piece.astype(jnp.float32) * scale).astype(jnp.bfloat16)
        weight_rows = lax.dynamic_slice_in_dim(enc_weight, feat_id * cols, cols, 0)
        part = jnp.dot(normed, weight_rows, preferred_element_type=jnp.float32)
        preact = part if preact is None else preact + part
    encode_preact = preact + enc_bias
    features = (encode_preact * jax.nn.sigmoid((encode_preact - threshold) / smooth_width)).astype(
        jnp.bfloat16
    )
    partial_value = jnp.dot(features, probe_weight, preferred_element_type=jnp.float32)
    num_tokens = features.shape[0]
    share_rows = num_tokens // lax.axis_size(("feat", "tok"))
    position = lax.axis_index(("feat", "tok"))
    class_ids = jnp.arange(probe_weight.shape[1], dtype=jnp.int32)
    logits = reduce_sum(partial_value)
    softmax_logits = logits + probe_bias
    exps = jnp.exp(softmax_logits)
    totals = jnp.sum(exps, axis=1, keepdims=True)
    onehot = (labels[:, None] == class_ids[None, :]).astype(jnp.float32)
    losses = jnp.log(totals[:, 0]) - jnp.sum(onehot * softmax_logits, axis=1)
    delta = (exps / totals - onehot).astype(jnp.bfloat16)
    token_loss = lax.dynamic_slice_in_dim(losses, position * share_rows, share_rows, 0)
    gradient = jnp.dot(features.T, delta, preferred_element_type=jnp.float32)
    return (gradient, token_loss)


def solution(mesh):
    in_specs = (
        P("tok", "feat"),
        P(None, ("feat", "tok")),
        P(("feat", "tok")),
        P(("feat", "tok")),
        P(("feat", "tok"), None),
        P(),
        P(),
    )
    out_specs = (P(("feat", "tok"), None), P(("feat", "tok")))
    return jax.shard_map(local, mesh=mesh, in_specs=in_specs, out_specs=out_specs, check_vma=False)
```

```python
import jax
import jax.numpy as jnp
from jax import lax
from jax.sharding import PartitionSpec as P

epsilon = 1e-06
smooth_width = 0.125


def exchange(value, axis, offset):
    size = lax.axis_size(axis)
    return lax.ppermute(value, axis, [(i, i ^ offset) for i in range(size)])


def tok_partners():
    return list(range(1, lax.axis_size("tok")))


def chip_partners():
    return list(range(2, lax.axis_size("feat"), 2))


def gather_pieces(block):
    rows, cols = block.shape
    my_tok = lax.axis_index("tok")
    my_feat = lax.axis_index("feat")
    column = block
    tok_bits = lax.axis_size("tok").bit_length() - 1
    for bit in range(tok_bits):
        got = exchange(column, "tok", 1 << bit)
        first = ((my_tok >> bit) & 1) == 0
        column = jnp.concatenate([jnp.where(first, column, got), jnp.where(first, got, column)])
    mine = [(my_feat, column)]
    for k in chip_partners():
        mine.append((my_feat ^ k, exchange(column, "feat", k)))
    bundle = exchange(jnp.stack([piece for _, piece in mine]), "feat", 1)
    pieces = list(mine)
    for j, k in enumerate([0] + chip_partners()):
        pieces.append((my_feat ^ 1 ^ k, bundle[j]))
    return pieces


def reduce_sum(value):
    total = value
    for k in tok_partners():
        total = total + exchange(value, "tok", k)
    value = total
    total = value
    for k in chip_partners():
        total = total + exchange(value, "feat", k)
    value = total
    return value + exchange(value, "feat", 1)


def local(residual, enc_weight, enc_bias, threshold, probe_weight, probe_bias, labels):
    rows, cols = residual.shape
    pieces = gather_pieces(residual)
    full_width = cols * lax.axis_size("feat")
    square_sum = None
    for _, piece in pieces:
        values = piece.astype(jnp.float32)
        part = jnp.sum(values * values, axis=1)
        square_sum = part if square_sum is None else square_sum + part
    scale = lax.rsqrt(square_sum / full_width + epsilon)[:, None]
    preact = None
    for feat_id, piece in pieces:
        normed = (piece.astype(jnp.float32) * scale).astype(jnp.bfloat16)
        weight_rows = lax.dynamic_slice_in_dim(enc_weight, feat_id * cols, cols, 0)
        part = jnp.dot(normed, weight_rows, preferred_element_type=jnp.float32)
        preact = part if preact is None else preact + part
    encode_preact = preact + enc_bias
    features = (encode_preact * jax.nn.sigmoid((encode_preact - threshold) / smooth_width)).astype(
        jnp.bfloat16
    )
    partial_value = jnp.dot(features, probe_weight, preferred_element_type=jnp.float32)
    num_tokens = features.shape[0]
    share_rows = num_tokens // lax.axis_size(("feat", "tok"))
    position = lax.axis_index(("feat", "tok"))
    class_ids = jnp.arange(probe_weight.shape[1], dtype=jnp.int32)
    logits = reduce_sum(partial_value)
    softmax_logits = logits + probe_bias
    exps = jnp.exp(softmax_logits)
    totals = jnp.sum(exps, axis=1, keepdims=True)
    onehot = (labels[:, None] == class_ids[None, :]).astype(jnp.float32)
    losses = jnp.log(totals[:, 0]) - jnp.sum(onehot * softmax_logits, axis=1)
    delta = (exps / totals - onehot).astype(jnp.bfloat16)
    token_loss = lax.dynamic_slice_in_dim(losses, position * share_rows, share_rows, 0)
    gradient = jnp.dot(features.T, delta, preferred_element_type=jnp.float32)
    return (gradient, token_loss)


def solution(mesh):
    in_specs = (
        P("tok", "feat"),
        P(None, ("feat", "tok")),
        P(("feat", "tok")),
        P(("feat", "tok")),
        P(("feat", "tok"), None),
        P(),
        P(),
    )
    out_specs = (P(("feat", "tok"), None), P(("feat", "tok")))
    return jax.shard_map(local, mesh=mesh, in_specs=in_specs, out_specs=out_specs, check_vma=False)
```

```python
import jax
import jax.numpy as jnp
from jax import lax
from jax.sharding import PartitionSpec as P
from jax.experimental import pallas as pl
from jax.experimental.pallas import tpu as pltpu

epsilon = 1e-06
smooth_width = 0.125


def exchange(value, axis, offset):
    size = lax.axis_size(axis)
    return lax.ppermute(value, axis, [(i, i ^ offset) for i in range(size)])


def tok_partners():
    return list(range(1, lax.axis_size("tok")))


def chip_partners():
    return list(range(2, lax.axis_size("feat"), 2))


def gather_pieces(block):
    rows, cols = block.shape
    my_tok = lax.axis_index("tok")
    my_feat = lax.axis_index("feat")
    column = block
    tok_bits = lax.axis_size("tok").bit_length() - 1
    for bit in range(tok_bits):
        got = exchange(column, "tok", 1 << bit)
        first = ((my_tok >> bit) & 1) == 0
        column = jnp.concatenate([jnp.where(first, column, got), jnp.where(first, got, column)])
    mine = [(my_feat, column)]
    for k in chip_partners():
        mine.append((my_feat ^ k, exchange(column, "feat", k)))
    own = jnp.stack([piece for _, piece in mine])
    other = exchange(own, "feat", 1)
    ids = [feat_id for feat_id, _ in mine] + [my_feat ^ 1 ^ k for k in [0] + chip_partners()]
    return own, other, jnp.stack(ids).astype(jnp.int32)


def encode_kernel(ids_ref, own_ref, other_ref, w_ref, b_ref, th_ref, pw_ref, feat_ref, part_ref):
    count, _, cols = own_ref.shape
    full_width = cols * 2 * count
    square_sum = None
    for ref in (own_ref, other_ref):
        for j in range(count):
            values = ref[j].astype(jnp.float32)
            part = jnp.sum(values * values, axis=1, keepdims=True)
            square_sum = part if square_sum is None else square_sum + part
    scale = lax.rsqrt(square_sum / full_width + epsilon)
    preact = None
    for half, ref in enumerate((own_ref, other_ref)):
        for j in range(count):
            normed = (ref[j].astype(jnp.float32) * scale).astype(jnp.bfloat16)
            start = pl.multiple_of(ids_ref[half * count + j] * cols, 16)
            weight_rows = w_ref[pl.ds(start, cols), :]
            part = jnp.dot(normed, weight_rows, preferred_element_type=jnp.float32)
            preact = part if preact is None else preact + part
    encode_preact = preact + b_ref[...]
    gate = jax.nn.sigmoid((encode_preact - th_ref[...]) / smooth_width)
    features = (encode_preact * gate).astype(jnp.bfloat16)
    feat_ref[...] = features
    part_ref[...] = jnp.dot(features, pw_ref[...], preferred_element_type=jnp.float32)


def encode(ids, own, other, enc_weight, enc_bias, threshold, probe_weight):
    tokens = own.shape[1]
    width = enc_weight.shape[1]
    vmem = pl.BlockSpec(memory_space=pltpu.VMEM)
    return pl.pallas_call(
        encode_kernel,
        out_shape=(
            jax.ShapeDtypeStruct((tokens, width), jnp.bfloat16),
            jax.ShapeDtypeStruct((tokens, probe_weight.shape[1]), jnp.float32),
        ),
        in_specs=[pl.BlockSpec(memory_space=pltpu.SMEM)] + [vmem] * 6,
        out_specs=(vmem, vmem),
        compiler_params=pltpu.CompilerParams(vmem_limit_bytes=60 * 1024 * 1024),
    )(ids, own, other, enc_weight, enc_bias.reshape(1, -1), threshold.reshape(1, -1), probe_weight)


def reduce_sum(value):
    total = value
    for k in tok_partners():
        total = total + exchange(value, "tok", k)
    value = total
    total = value
    for k in chip_partners():
        total = total + exchange(value, "feat", k)
    value = total
    return value + exchange(value, "feat", 1)


def local(residual, enc_weight, enc_bias, threshold, probe_weight, probe_bias, labels):
    rows, cols = residual.shape
    own, other, ids = gather_pieces(residual)
    features, partial_value = encode(ids, own, other, enc_weight, enc_bias, threshold, probe_weight)
    num_tokens = features.shape[0]
    share_rows = num_tokens // lax.axis_size(("feat", "tok"))
    position = lax.axis_index(("feat", "tok"))
    class_ids = jnp.arange(probe_weight.shape[1], dtype=jnp.int32)
    logits = reduce_sum(partial_value)
    softmax_logits = logits + probe_bias
    exps = jnp.exp(softmax_logits)
    totals = jnp.sum(exps, axis=1, keepdims=True)
    onehot = (labels[:, None] == class_ids[None, :]).astype(jnp.float32)
    losses = jnp.log(totals[:, 0]) - jnp.sum(onehot * softmax_logits, axis=1)
    delta = (exps / totals - onehot).astype(jnp.bfloat16)
    token_loss = lax.dynamic_slice_in_dim(losses, position * share_rows, share_rows, 0)
    gradient = jnp.dot(features.T, delta, preferred_element_type=jnp.float32)
    return (gradient, token_loss)


def solution(mesh):
    in_specs = (
        P("tok", "feat"),
        P(None, ("feat", "tok")),
        P(("feat", "tok")),
        P(("feat", "tok")),
        P(("feat", "tok"), None),
        P(),
        P(),
    )
    out_specs = (P(("feat", "tok"), None), P(("feat", "tok")))
    return jax.shard_map(local, mesh=mesh, in_specs=in_specs, out_specs=out_specs, check_vma=False)
```

```python
import jax
import jax.numpy as jnp
from jax import lax
from jax.sharding import PartitionSpec as P

epsilon = 1e-06
smooth_width = 0.125


def exchange(value, axis, offset):
    size = lax.axis_size(axis)
    return lax.ppermute(value, axis, [(i, i ^ offset) for i in range(size)])


def tok_partners():
    return list(range(1, lax.axis_size("tok")))


def chip_partners():
    return list(range(2, lax.axis_size("feat"), 2))


def ordered(bit_set, mine, got, axis):
    first = jnp.logical_not(bit_set)
    return jnp.concatenate([jnp.where(first, mine, got), jnp.where(first, got, mine)], axis=axis)


def gather_half(block):
    rows, cols = block.shape
    half = rows // 2
    my_tok = lax.axis_index("tok")
    my_feat = lax.axis_index("feat")
    core = my_feat & 1
    keep = lax.dynamic_slice_in_dim(block, core * half, half, 0)
    send = lax.dynamic_slice_in_dim(block, (1 - core) * half, half, 0)
    got = exchange(send, "feat", 1)
    held = jnp.stack([keep, got])
    tok_bits = lax.axis_size("tok").bit_length() - 1
    for bit in range(tok_bits):
        other = exchange(held, "tok", 1 << bit)
        held = ordered((my_tok >> bit) & 1, held, other, 1)
    pieces = [((my_feat, my_feat ^ 1), held)]
    for k in chip_partners():
        pieces.append(((my_feat ^ k, my_feat ^ k ^ 1), exchange(held, "feat", k)))
    return pieces


def reduce_sum(value):
    total = value
    for k in tok_partners():
        total = total + exchange(value, "tok", k)
    value = total
    total = value
    for k in chip_partners():
        total = total + exchange(value, "feat", k)
    return total


def local(residual, enc_weight, enc_bias, threshold, probe_weight, probe_bias, labels):
    rows, cols = residual.shape
    half = rows // 2
    feat_size = lax.axis_size("feat")
    tok_size = lax.axis_size("tok")
    assert feat_size == 2 * tok_size and rows % 2 == 0
    my_feat = lax.axis_index("feat")
    core = my_feat & 1
    pieces = gather_half(residual)
    weight_both = jnp.concatenate([enc_weight, exchange(enc_weight, "feat", 1)], axis=1)
    gate_params = jnp.stack([enc_bias, threshold])
    gate_both = jnp.concatenate([gate_params, exchange(gate_params, "feat", 1)], axis=1)
    probe_both = jnp.concatenate([probe_weight, exchange(probe_weight, "feat", 1)], axis=0)
    full_width = cols * feat_size
    square_sum = None
    for _, piece in pieces:
        values = piece.astype(jnp.float32)
        part = jnp.sum(values * values, axis=(0, 2))
        square_sum = part if square_sum is None else square_sum + part
    scale = lax.rsqrt(square_sum / full_width + epsilon)[:, None]
    preact = None
    for feat_ids, piece in pieces:
        for g in range(2):
            normed = (piece[g].astype(jnp.float32) * scale).astype(jnp.bfloat16)
            weight_rows = lax.dynamic_slice_in_dim(weight_both, feat_ids[g] * cols, cols, 0)
            part = jnp.dot(normed, weight_rows, preferred_element_type=jnp.float32)
            preact = part if preact is None else preact + part
    encode_preact = preact + gate_both[0]
    features = (encode_preact * jax.nn.sigmoid((encode_preact - gate_both[1]) / smooth_width)).astype(
        jnp.bfloat16
    )
    partial_value = jnp.dot(features, probe_both, preferred_element_type=jnp.float32)
    logits = reduce_sum(partial_value)
    classes = probe_weight.shape[1]
    class_ids = jnp.arange(classes, dtype=jnp.int32)
    my_labels = lax.dynamic_slice_in_dim(labels.reshape(tok_size, rows), core * half, half, 1).reshape(-1)
    softmax_logits = logits + probe_bias
    exps = jnp.exp(softmax_logits)
    totals = jnp.sum(exps, axis=1, keepdims=True)
    onehot = (my_labels[:, None] == class_ids[None, :]).astype(jnp.float32)
    losses = jnp.log(totals[:, 0]) - jnp.sum(onehot * softmax_logits, axis=1)
    delta = (exps / totals - onehot).astype(jnp.bfloat16)
    num_tokens = tok_size * rows
    share_rows = num_tokens // (feat_size * tok_size)
    start = lax.axis_index(("feat", "tok")) * share_rows
    token_loss = lax.dynamic_slice_in_dim(
        losses, (start // rows) * half + start % rows - core * half, share_rows, 0
    )
    gradient_both = jnp.dot(features.T, delta, preferred_element_type=jnp.float32)
    width = enc_weight.shape[1]
    gradient = gradient_both[:width] + exchange(gradient_both[width:], "feat", 1)
    return (gradient, token_loss)


def solution(mesh):
    in_specs = (
        P("tok", "feat"),
        P(None, ("feat", "tok")),
        P(("feat", "tok")),
        P(("feat", "tok")),
        P(("feat", "tok"), None),
        P(),
        P(),
    )
    out_specs = (P(("feat", "tok"), None), P(("feat", "tok")))
    return jax.shard_map(local, mesh=mesh, in_specs=in_specs, out_specs=out_specs, check_vma=False)
```

```python
import jax
import jax.numpy as jnp
from jax import lax
from jax.sharding import PartitionSpec as P

epsilon = 1e-06
smooth_width = 0.125


def exchange(value, axis, offset):
    size = lax.axis_size(axis)
    return lax.ppermute(value, axis, [(i, i ^ offset) for i in range(size)])


def tok_partners():
    return list(range(1, lax.axis_size("tok")))


def chip_partners():
    return list(range(2, lax.axis_size("feat"), 2))


def ordered(bit_set, mine, got, axis):
    first = jnp.logical_not(bit_set)
    return jnp.concatenate([jnp.where(first, mine, got), jnp.where(first, got, mine)], axis=axis)


def gather_half(block):
    rows, cols = block.shape
    half = rows // 2
    my_tok = lax.axis_index("tok")
    my_feat = lax.axis_index("feat")
    core = my_feat & 1
    keep = lax.dynamic_slice_in_dim(block, core * half, half, 0)
    send = lax.dynamic_slice_in_dim(block, (1 - core) * half, half, 0)
    got = exchange(send, "feat", 1)
    held = ordered(core, keep, got, 1)
    tok_bits = lax.axis_size("tok").bit_length() - 1
    for bit in range(tok_bits):
        other = exchange(held, "tok", 1 << bit)
        held = ordered((my_tok >> bit) & 1, held, other, 0)
    my_chip = my_feat >> 1
    pieces = [(my_chip, held)]
    for k in chip_partners():
        pieces.append((my_chip ^ (k >> 1), exchange(held, "feat", k)))
    return pieces


def reduce_sum(value):
    total = value
    for k in tok_partners():
        total = total + exchange(value, "tok", k)
    value = total
    total = value
    for k in chip_partners():
        total = total + exchange(value, "feat", k)
    return total


def local(residual, enc_weight, enc_bias, threshold, probe_weight, probe_bias, labels):
    rows, cols = residual.shape
    half = rows // 2
    feat_size = lax.axis_size("feat")
    tok_size = lax.axis_size("tok")
    assert feat_size == 2 * tok_size and rows % 2 == 0
    my_feat = lax.axis_index("feat")
    core = my_feat & 1
    pieces = gather_half(residual)
    other_weight = exchange(enc_weight, "feat", 1)
    other_gate = exchange(jnp.stack([enc_bias, threshold]), "feat", 1)
    other_probe = exchange(probe_weight, "feat", 1)
    full_width = cols * feat_size
    square_sum = None
    for _, piece in pieces:
        values = piece.astype(jnp.float32)
        part = jnp.sum(values * values, axis=1)
        square_sum = part if square_sum is None else square_sum + part
    scale = lax.rsqrt(square_sum / full_width + epsilon)[:, None]
    preact = [None, None]
    for chip, piece in pieces:
        normed = (piece.astype(jnp.float32) * scale).astype(jnp.bfloat16)
        for g, weight in enumerate((enc_weight, other_weight)):
            weight_rows = lax.dynamic_slice_in_dim(weight, chip * 2 * cols, 2 * cols, 0)
            part = jnp.dot(normed, weight_rows, preferred_element_type=jnp.float32)
            preact[g] = part if preact[g] is None else preact[g] + part
    gates = ((enc_bias, threshold), (other_gate[0], other_gate[1]))
    features = []
    for g in range(2):
        encode_preact = preact[g] + gates[g][0]
        gate = jax.nn.sigmoid((encode_preact - gates[g][1]) / smooth_width)
        features.append((encode_preact * gate).astype(jnp.bfloat16))
    partial_value = jnp.dot(features[0], probe_weight, preferred_element_type=jnp.float32)
    partial_value = partial_value + jnp.dot(features[1], other_probe, preferred_element_type=jnp.float32)
    logits = reduce_sum(partial_value)
    classes = probe_weight.shape[1]
    class_ids = jnp.arange(classes, dtype=jnp.int32)
    my_labels = lax.dynamic_slice_in_dim(labels.reshape(tok_size, rows), core * half, half, 1).reshape(-1)
    softmax_logits = logits + probe_bias
    exps = jnp.exp(softmax_logits)
    totals = jnp.sum(exps, axis=1, keepdims=True)
    onehot = (my_labels[:, None] == class_ids[None, :]).astype(jnp.float32)
    losses = jnp.log(totals[:, 0]) - jnp.sum(onehot * softmax_logits, axis=1)
    delta = (exps / totals - onehot).astype(jnp.bfloat16)
    num_tokens = tok_size * rows
    share_rows = num_tokens // (feat_size * tok_size)
    start = lax.axis_index(("feat", "tok")) * share_rows
    token_loss = lax.dynamic_slice_in_dim(
        losses, (start // rows) * half + start % rows - core * half, share_rows, 0
    )
    gradient = jnp.dot(features[0].T, delta, preferred_element_type=jnp.float32)
    gradient_other = jnp.dot(features[1].T, delta, preferred_element_type=jnp.float32)
    gradient = gradient + exchange(gradient_other, "feat", 1)
    return (gradient, token_loss)


def solution(mesh):
    in_specs = (
        P("tok", "feat"),
        P(None, ("feat", "tok")),
        P(("feat", "tok")),
        P(("feat", "tok")),
        P(("feat", "tok"), None),
        P(),
        P(),
    )
    out_specs = (P(("feat", "tok"), None), P(("feat", "tok")))
    return jax.shard_map(local, mesh=mesh, in_specs=in_specs, out_specs=out_specs, check_vma=False)
```

```python
import jax
import jax.numpy as jnp
from jax import lax
from jax.sharding import PartitionSpec as P

epsilon = 1e-06
smooth_width = 0.125


def exchange(value, axis, offset):
    size = lax.axis_size(axis)
    return lax.ppermute(value, axis, [(i, i ^ offset) for i in range(size)])


def tok_partners():
    return list(range(1, lax.axis_size("tok")))


def chip_partners():
    return list(range(2, lax.axis_size("feat"), 2))


def ordered(bit_set, mine, got, axis):
    first = jnp.logical_not(bit_set)
    return jnp.concatenate([jnp.where(first, mine, got), jnp.where(first, got, mine)], axis=axis)


def gather_half(block):
    rows, cols = block.shape
    half = rows // 2
    my_tok = lax.axis_index("tok")
    my_feat = lax.axis_index("feat")
    core = my_feat & 1
    keep = lax.dynamic_slice_in_dim(block, core * half, half, 0)
    send = lax.dynamic_slice_in_dim(block, (1 - core) * half, half, 0)
    got = exchange(send, "feat", 1)
    held = ordered(core, keep, got, 1)
    held = lax.all_gather(held, "tok", axis=0, tiled=True)
    my_chip = my_feat >> 1
    pieces = [(my_chip, held)]
    for k in chip_partners():
        pieces.append((my_chip ^ (k >> 1), exchange(held, "feat", k)))
    return pieces


def reduce_sum(value):
    total = value
    for k in tok_partners():
        total = total + exchange(value, "tok", k)
    value = total
    total = value
    for k in chip_partners():
        total = total + exchange(value, "feat", k)
    return total


def local(residual, enc_weight, enc_bias, threshold, probe_weight, probe_bias, labels):
    rows, cols = residual.shape
    half = rows // 2
    feat_size = lax.axis_size("feat")
    tok_size = lax.axis_size("tok")
    assert feat_size == 2 * tok_size and rows % 2 == 0
    my_feat = lax.axis_index("feat")
    core = my_feat & 1
    pieces = gather_half(residual)
    other_weight = exchange(enc_weight, "feat", 1)
    other_gate = exchange(jnp.stack([enc_bias, threshold]), "feat", 1)
    other_probe = exchange(probe_weight, "feat", 1)
    full_width = cols * feat_size
    square_sum = None
    for _, piece in pieces:
        values = piece.astype(jnp.float32)
        part = jnp.sum(values * values, axis=1)
        square_sum = part if square_sum is None else square_sum + part
    scale = lax.rsqrt(square_sum / full_width + epsilon)[:, None]
    preact = [None, None]
    for chip, piece in pieces:
        normed = (piece.astype(jnp.float32) * scale).astype(jnp.bfloat16)
        for g, weight in enumerate((enc_weight, other_weight)):
            weight_rows = lax.dynamic_slice_in_dim(weight, chip * 2 * cols, 2 * cols, 0)
            part = jnp.dot(normed, weight_rows, preferred_element_type=jnp.float32)
            preact[g] = part if preact[g] is None else preact[g] + part
    gates = ((enc_bias, threshold), (other_gate[0], other_gate[1]))
    features = []
    for g in range(2):
        encode_preact = preact[g] + gates[g][0]
        gate = jax.nn.sigmoid((encode_preact - gates[g][1]) / smooth_width)
        features.append((encode_preact * gate).astype(jnp.bfloat16))
    partial_value = jnp.dot(features[0], probe_weight, preferred_element_type=jnp.float32)
    partial_value = partial_value + jnp.dot(features[1], other_probe, preferred_element_type=jnp.float32)
    logits = reduce_sum(partial_value)
    classes = probe_weight.shape[1]
    class_ids = jnp.arange(classes, dtype=jnp.int32)
    my_labels = lax.dynamic_slice_in_dim(labels.reshape(tok_size, rows), core * half, half, 1).reshape(-1)
    softmax_logits = logits + probe_bias
    exps = jnp.exp(softmax_logits)
    totals = jnp.sum(exps, axis=1, keepdims=True)
    onehot = (my_labels[:, None] == class_ids[None, :]).astype(jnp.float32)
    losses = jnp.log(totals[:, 0]) - jnp.sum(onehot * softmax_logits, axis=1)
    delta = (exps / totals - onehot).astype(jnp.bfloat16)
    num_tokens = tok_size * rows
    share_rows = num_tokens // (feat_size * tok_size)
    start = lax.axis_index(("feat", "tok")) * share_rows
    token_loss = lax.dynamic_slice_in_dim(
        losses, (start // rows) * half + start % rows - core * half, share_rows, 0
    )
    gradient = jnp.dot(features[0].T, delta, preferred_element_type=jnp.float32)
    gradient_other = jnp.dot(features[1].T, delta, preferred_element_type=jnp.float32)
    gradient = gradient + exchange(gradient_other, "feat", 1)
    return (gradient, token_loss)


def solution(mesh):
    in_specs = (
        P("tok", "feat"),
        P(None, ("feat", "tok")),
        P(("feat", "tok")),
        P(("feat", "tok")),
        P(("feat", "tok"), None),
        P(),
        P(),
    )
    out_specs = (P(("feat", "tok"), None), P(("feat", "tok")))
    return jax.shard_map(local, mesh=mesh, in_specs=in_specs, out_specs=out_specs, check_vma=False)
```

```python
import jax
import jax.numpy as jnp
from jax import lax
from jax.sharding import PartitionSpec as P

epsilon = 1e-06
smooth_width = 0.125


def exchange(value, axis, offset):
    size = lax.axis_size(axis)
    return lax.ppermute(value, axis, [(i, i ^ offset) for i in range(size)])


def tok_partners():
    return list(range(1, lax.axis_size("tok")))


def chip_partners():
    return list(range(2, lax.axis_size("feat"), 2))


def ordered(bit_set, mine, got, axis):
    first = jnp.logical_not(bit_set)
    return jnp.concatenate([jnp.where(first, mine, got), jnp.where(first, got, mine)], axis=axis)


def gather_half(block):
    rows, cols = block.shape
    half = rows // 2
    my_tok = lax.axis_index("tok")
    my_feat = lax.axis_index("feat")
    core = my_feat & 1
    keep = lax.dynamic_slice_in_dim(block, core * half, half, 0)
    send = lax.dynamic_slice_in_dim(block, (1 - core) * half, half, 0)
    got = exchange(send, "feat", 1)
    held = ordered(core, keep, got, 1)
    tok_bits = lax.axis_size("tok").bit_length() - 1
    for bit in reversed(range(tok_bits)):
        other = exchange(held, "tok", 1 << bit)
        blocks = held.shape[0] // half
        first = ((my_tok >> bit) & 1) == 0
        low = jnp.where(first, held, other).reshape(blocks, half, -1)
        high = jnp.where(first, other, held).reshape(blocks, half, -1)
        held = jnp.stack([low, high], axis=1).reshape(2 * blocks * half, -1)
    my_chip = my_feat >> 1
    pieces = [(my_chip, held)]
    for k in chip_partners():
        pieces.append((my_chip ^ (k >> 1), exchange(held, "feat", k)))
    return pieces


def reduce_sum(value):
    total = value
    for k in tok_partners():
        total = total + exchange(value, "tok", k)
    value = total
    total = value
    for k in chip_partners():
        total = total + exchange(value, "feat", k)
    return total


def local(residual, enc_weight, enc_bias, threshold, probe_weight, probe_bias, labels):
    rows, cols = residual.shape
    half = rows // 2
    feat_size = lax.axis_size("feat")
    tok_size = lax.axis_size("tok")
    assert feat_size == 2 * tok_size and rows % 2 == 0
    my_feat = lax.axis_index("feat")
    core = my_feat & 1
    pieces = gather_half(residual)
    other_weight = exchange(enc_weight, "feat", 1)
    other_gate = exchange(jnp.stack([enc_bias, threshold]), "feat", 1)
    other_probe = exchange(probe_weight, "feat", 1)
    full_width = cols * feat_size
    square_sum = None
    for _, piece in pieces:
        values = piece.astype(jnp.float32)
        part = jnp.sum(values * values, axis=1)
        square_sum = part if square_sum is None else square_sum + part
    scale = lax.rsqrt(square_sum / full_width + epsilon)[:, None]
    preact = [None, None]
    for chip, piece in pieces:
        normed = (piece.astype(jnp.float32) * scale).astype(jnp.bfloat16)
        for g, weight in enumerate((enc_weight, other_weight)):
            weight_rows = lax.dynamic_slice_in_dim(weight, chip * 2 * cols, 2 * cols, 0)
            part = jnp.dot(normed, weight_rows, preferred_element_type=jnp.float32)
            preact[g] = part if preact[g] is None else preact[g] + part
    gates = ((enc_bias, threshold), (other_gate[0], other_gate[1]))
    features = []
    for g in range(2):
        encode_preact = preact[g] + gates[g][0]
        gate = jax.nn.sigmoid((encode_preact - gates[g][1]) / smooth_width)
        features.append((encode_preact * gate).astype(jnp.bfloat16))
    partial_value = jnp.dot(features[0], probe_weight, preferred_element_type=jnp.float32)
    partial_value = partial_value + jnp.dot(features[1], other_probe, preferred_element_type=jnp.float32)
    logits = reduce_sum(partial_value)
    classes = probe_weight.shape[1]
    class_ids = jnp.arange(classes, dtype=jnp.int32)
    my_labels = lax.dynamic_slice_in_dim(labels.reshape(tok_size, rows), core * half, half, 1).reshape(-1)
    softmax_logits = logits + probe_bias
    exps = jnp.exp(softmax_logits)
    totals = jnp.sum(exps, axis=1, keepdims=True)
    onehot = (my_labels[:, None] == class_ids[None, :]).astype(jnp.float32)
    losses = jnp.log(totals[:, 0]) - jnp.sum(onehot * softmax_logits, axis=1)
    delta = (exps / totals - onehot).astype(jnp.bfloat16)
    num_tokens = tok_size * rows
    share_rows = num_tokens // (feat_size * tok_size)
    start = lax.axis_index(("feat", "tok")) * share_rows
    token_loss = lax.dynamic_slice_in_dim(
        losses, (start // rows) * half + start % rows - core * half, share_rows, 0
    )
    gradient = jnp.dot(features[0].T, delta, preferred_element_type=jnp.float32)
    gradient_other = jnp.dot(features[1].T, delta, preferred_element_type=jnp.float32)
    gradient = gradient + exchange(gradient_other, "feat", 1)
    return (gradient, token_loss)


def solution(mesh):
    in_specs = (
        P("tok", "feat"),
        P(None, ("feat", "tok")),
        P(("feat", "tok")),
        P(("feat", "tok")),
        P(("feat", "tok"), None),
        P(),
        P(),
    )
    out_specs = (P(("feat", "tok"), None), P(("feat", "tok")))
    return jax.shard_map(local, mesh=mesh, in_specs=in_specs, out_specs=out_specs, check_vma=False)
```

```python
import jax
import jax.numpy as jnp
from jax import lax
from jax.sharding import PartitionSpec as P

epsilon = 1e-06
smooth_width = 0.125


def exchange(value, axis, offset):
    size = lax.axis_size(axis)
    return lax.ppermute(value, axis, [(i, i ^ offset) for i in range(size)])


def tok_partners():
    return list(range(1, lax.axis_size("tok")))


def chip_partners():
    return list(range(2, lax.axis_size("feat"), 2))


def ordered(bit_set, mine, got, axis):
    first = jnp.logical_not(bit_set)
    return jnp.concatenate([jnp.where(first, mine, got), jnp.where(first, got, mine)], axis=axis)


def tok_bits_of():
    return lax.axis_size("tok").bit_length() - 1


def reverse_bits(value, count):
    out = 0 * value
    for i in range(count):
        out = out + (((value >> i) & 1) << (count - 1 - i))
    return out


def gather_half(block):
    rows, cols = block.shape
    half = rows // 2
    my_tok = lax.axis_index("tok")
    my_feat = lax.axis_index("feat")
    core = my_feat & 1
    keep = lax.dynamic_slice_in_dim(block, core * half, half, 0)
    send = lax.dynamic_slice_in_dim(block, (1 - core) * half, half, 0)
    got = exchange(send, "feat", 1)
    held = ordered(core, keep, got, 1)
    for bit in reversed(range(tok_bits_of())):
        other = exchange(held, "tok", 1 << bit)
        held = ordered((my_tok >> bit) & 1, held, other, 0)
    my_chip = my_feat >> 1
    pieces = [(my_chip, held)]
    for k in chip_partners():
        pieces.append((my_chip ^ (k >> 1), exchange(held, "feat", k)))
    return pieces


def reduce_sum(value):
    total = value
    for k in tok_partners():
        total = total + exchange(value, "tok", k)
    value = total
    total = value
    for k in chip_partners():
        total = total + exchange(value, "feat", k)
    return total


def local(residual, enc_weight, enc_bias, threshold, probe_weight, probe_bias, labels):
    rows, cols = residual.shape
    half = rows // 2
    feat_size = lax.axis_size("feat")
    tok_size = lax.axis_size("tok")
    assert feat_size == 2 * tok_size and rows % 2 == 0
    my_feat = lax.axis_index("feat")
    core = my_feat & 1
    pieces = gather_half(residual)
    other_weight = exchange(enc_weight, "feat", 1)
    other_gate = exchange(jnp.stack([enc_bias, threshold]), "feat", 1)
    other_probe = exchange(probe_weight, "feat", 1)
    full_width = cols * feat_size
    square_sum = None
    for _, piece in pieces:
        values = piece.astype(jnp.float32)
        part = jnp.sum(values * values, axis=1)
        square_sum = part if square_sum is None else square_sum + part
    scale = lax.rsqrt(square_sum / full_width + epsilon)[:, None]
    preact = [None, None]
    for chip, piece in pieces:
        normed = (piece.astype(jnp.float32) * scale).astype(jnp.bfloat16)
        for g, weight in enumerate((enc_weight, other_weight)):
            weight_rows = lax.dynamic_slice_in_dim(weight, chip * 2 * cols, 2 * cols, 0)
            part = jnp.dot(normed, weight_rows, preferred_element_type=jnp.float32)
            preact[g] = part if preact[g] is None else preact[g] + part
    gates = ((enc_bias, threshold), (other_gate[0], other_gate[1]))
    features = []
    for g in range(2):
        encode_preact = preact[g] + gates[g][0]
        gate = jax.nn.sigmoid((encode_preact - gates[g][1]) / smooth_width)
        features.append((encode_preact * gate).astype(jnp.bfloat16))
    partial_value = jnp.dot(features[0], probe_weight, preferred_element_type=jnp.float32)
    partial_value = partial_value + jnp.dot(features[1], other_probe, preferred_element_type=jnp.float32)
    logits = reduce_sum(partial_value)
    classes = probe_weight.shape[1]
    class_ids = jnp.arange(classes, dtype=jnp.int32)
    bits = tok_bits_of()
    block_order = [reverse_bits(p, bits) for p in range(tok_size)]
    label_rows = labels.reshape(tok_size, rows)[jnp.array(block_order, jnp.int32)]
    my_labels = lax.dynamic_slice_in_dim(label_rows, core * half, half, 1).reshape(-1)
    softmax_logits = logits + probe_bias
    exps = jnp.exp(softmax_logits)
    totals = jnp.sum(exps, axis=1, keepdims=True)
    onehot = (my_labels[:, None] == class_ids[None, :]).astype(jnp.float32)
    losses = jnp.log(totals[:, 0]) - jnp.sum(onehot * softmax_logits, axis=1)
    delta = (exps / totals - onehot).astype(jnp.bfloat16)
    num_tokens = tok_size * rows
    share_rows = num_tokens // (feat_size * tok_size)
    start = lax.axis_index(("feat", "tok")) * share_rows
    token_loss = lax.dynamic_slice_in_dim(
        losses, reverse_bits(start // rows, bits) * half + start % rows - core * half, share_rows, 0
    )
    gradient = jnp.dot(features[0].T, delta, preferred_element_type=jnp.float32)
    gradient_other = jnp.dot(features[1].T, delta, preferred_element_type=jnp.float32)
    gradient = gradient + exchange(gradient_other, "feat", 1)
    return (gradient, token_loss)


def solution(mesh):
    in_specs = (
        P("tok", "feat"),
        P(None, ("feat", "tok")),
        P(("feat", "tok")),
        P(("feat", "tok")),
        P(("feat", "tok"), None),
        P(),
        P(),
    )
    out_specs = (P(("feat", "tok"), None), P(("feat", "tok")))
    return jax.shard_map(local, mesh=mesh, in_specs=in_specs, out_specs=out_specs, check_vma=False)
```

```python
import jax
import jax.numpy as jnp
from jax import lax
from jax.sharding import PartitionSpec as P

epsilon = 1e-06
smooth_width = 0.125


def exchange(value, axis, offset):
    size = lax.axis_size(axis)
    return lax.ppermute(value, axis, [(i, i ^ offset) for i in range(size)])


def tok_partners():
    return list(range(1, lax.axis_size("tok")))


def chip_partners():
    return list(range(2, lax.axis_size("feat"), 2))


def ordered(bit_set, mine, got, axis):
    first = jnp.logical_not(bit_set)
    return jnp.concatenate([jnp.where(first, mine, got), jnp.where(first, got, mine)], axis=axis)


def tok_bits_of():
    return lax.axis_size("tok").bit_length() - 1


def reverse_bits(value, count):
    out = 0 * value
    for i in range(count):
        out = out + (((value >> i) & 1) << (count - 1 - i))
    return out


def gather_half(block):
    rows, cols = block.shape
    half = rows // 2
    my_tok = lax.axis_index("tok")
    my_feat = lax.axis_index("feat")
    core = my_feat & 1
    keep = lax.dynamic_slice_in_dim(block, core * half, half, 0)
    send = lax.dynamic_slice_in_dim(block, (1 - core) * half, half, 0)
    got = exchange(send, "feat", 1)
    held = ordered(core, keep, got, 1)
    for bit in reversed(range(tok_bits_of())):
        other = exchange(held, "tok", 1 << bit)
        held = ordered((my_tok >> bit) & 1, held, other, 0)
    my_chip = my_feat >> 1
    pieces = [(my_chip, held)]
    for k in chip_partners():
        pieces.append((my_chip ^ (k >> 1), exchange(held, "feat", k)))
    return pieces


def row_scales(block):
    rows, cols = block.shape
    half = rows // 2
    my_tok = lax.axis_index("tok")
    core = lax.axis_index("feat") & 1
    values = block.astype(jnp.float32)
    sums = jnp.sum(values * values, axis=1)
    total = sums
    for k in chip_partners():
        total = total + exchange(sums, "feat", k)
    total = total + exchange(total, "feat", 1)
    held = lax.dynamic_slice_in_dim(total, core * half, half, 0)
    for bit in reversed(range(tok_bits_of())):
        other = exchange(held, "tok", 1 << bit)
        held = ordered((my_tok >> bit) & 1, held, other, 0)
    full_width = cols * lax.axis_size("feat")
    return lax.rsqrt(held / full_width + epsilon)[:, None]


def reduce_sum(value):
    total = value
    for k in tok_partners():
        total = total + exchange(value, "tok", k)
    value = total
    total = value
    for k in chip_partners():
        total = total + exchange(value, "feat", k)
    return total


def local(residual, enc_weight, enc_bias, threshold, probe_weight, probe_bias, labels):
    rows, cols = residual.shape
    half = rows // 2
    feat_size = lax.axis_size("feat")
    tok_size = lax.axis_size("tok")
    assert feat_size == 2 * tok_size and rows % 2 == 0
    my_feat = lax.axis_index("feat")
    core = my_feat & 1
    pieces = gather_half(residual)
    other_weight = exchange(enc_weight, "feat", 1)
    other_gate = exchange(jnp.stack([enc_bias, threshold]), "feat", 1)
    other_probe = exchange(probe_weight, "feat", 1)
    scale = row_scales(residual)
    preact = [None, None]
    for chip, piece in pieces:
        normed = (piece.astype(jnp.float32) * scale).astype(jnp.bfloat16)
        for g, weight in enumerate((enc_weight, other_weight)):
            weight_rows = lax.dynamic_slice_in_dim(weight, chip * 2 * cols, 2 * cols, 0)
            part = jnp.dot(normed, weight_rows, preferred_element_type=jnp.float32)
            preact[g] = part if preact[g] is None else preact[g] + part
    gates = ((enc_bias, threshold), (other_gate[0], other_gate[1]))
    features = []
    for g in range(2):
        encode_preact = preact[g] + gates[g][0]
        gate = jax.nn.sigmoid((encode_preact - gates[g][1]) / smooth_width)
        features.append((encode_preact * gate).astype(jnp.bfloat16))
    partial_value = jnp.dot(features[0], probe_weight, preferred_element_type=jnp.float32)
    partial_value = partial_value + jnp.dot(features[1], other_probe, preferred_element_type=jnp.float32)
    logits = reduce_sum(partial_value)
    classes = probe_weight.shape[1]
    class_ids = jnp.arange(classes, dtype=jnp.int32)
    bits = tok_bits_of()
    block_order = [reverse_bits(p, bits) for p in range(tok_size)]
    label_rows = labels.reshape(tok_size, rows)[jnp.array(block_order, jnp.int32)]
    my_labels = lax.dynamic_slice_in_dim(label_rows, core * half, half, 1).reshape(-1)
    softmax_logits = logits + probe_bias
    exps = jnp.exp(softmax_logits)
    totals = jnp.sum(exps, axis=1, keepdims=True)
    onehot = (my_labels[:, None] == class_ids[None, :]).astype(jnp.float32)
    losses = jnp.log(totals[:, 0]) - jnp.sum(onehot * softmax_logits, axis=1)
    delta = (exps / totals - onehot).astype(jnp.bfloat16)
    num_tokens = tok_size * rows
    share_rows = num_tokens // (feat_size * tok_size)
    start = lax.axis_index(("feat", "tok")) * share_rows
    token_loss = lax.dynamic_slice_in_dim(
        losses, reverse_bits(start // rows, bits) * half + start % rows - core * half, share_rows, 0
    )
    gradient = jnp.dot(features[0].T, delta, preferred_element_type=jnp.float32)
    gradient_other = jnp.dot(features[1].T, delta, preferred_element_type=jnp.float32)
    gradient = gradient + exchange(gradient_other, "feat", 1)
    return (gradient, token_loss)


def solution(mesh):
    in_specs = (
        P("tok", "feat"),
        P(None, ("feat", "tok")),
        P(("feat", "tok")),
        P(("feat", "tok")),
        P(("feat", "tok"), None),
        P(),
        P(),
    )
    out_specs = (P(("feat", "tok"), None), P(("feat", "tok")))
    return jax.shard_map(local, mesh=mesh, in_specs=in_specs, out_specs=out_specs, check_vma=False)
```

```python
import jax
import jax.numpy as jnp
from jax import lax
from jax.sharding import PartitionSpec as P

epsilon = 1e-06
smooth_width = 0.125


def exchange(value, axis, offset):
    size = lax.axis_size(axis)
    return lax.ppermute(value, axis, [(i, i ^ offset) for i in range(size)])


def tok_partners():
    return list(range(1, lax.axis_size("tok")))


def chip_partners():
    return list(range(2, lax.axis_size("feat"), 2))


def ordered(bit_set, mine, got, axis):
    first = jnp.logical_not(bit_set)
    return jnp.concatenate([jnp.where(first, mine, got), jnp.where(first, got, mine)], axis=axis)


def gather_half(block):
    rows, cols = block.shape
    half = rows // 2
    my_tok = lax.axis_index("tok")
    my_feat = lax.axis_index("feat")
    core = my_feat & 1
    keep = lax.dynamic_slice_in_dim(block, core * half, half, 0)
    send = lax.dynamic_slice_in_dim(block, (1 - core) * half, half, 0)
    got = exchange(send, "feat", 1)
    held = ordered(core, keep, got, 1)
    tok_bits = lax.axis_size("tok").bit_length() - 1
    pieces = [held] + [exchange(held, "tok", k) for k in tok_partners()]
    held = jnp.concatenate(pieces, axis=0)
    width = held.shape[1]
    held = held.reshape([2] * tok_bits + [half, width])
    for bit in range(tok_bits):
        axis = tok_bits - 1 - bit
        held = jnp.where(((my_tok >> bit) & 1) == 1, jnp.flip(held, axis=axis), held)
    held = held.reshape(-1, width)
    my_chip = my_feat >> 1
    pieces = [(my_chip, held)]
    for k in chip_partners():
        pieces.append((my_chip ^ (k >> 1), exchange(held, "feat", k)))
    return pieces


def reduce_sum(value):
    total = value
    for k in tok_partners():
        total = total + exchange(value, "tok", k)
    value = total
    total = value
    for k in chip_partners():
        total = total + exchange(value, "feat", k)
    return total


def local(residual, enc_weight, enc_bias, threshold, probe_weight, probe_bias, labels):
    rows, cols = residual.shape
    half = rows // 2
    feat_size = lax.axis_size("feat")
    tok_size = lax.axis_size("tok")
    assert feat_size == 2 * tok_size and rows % 2 == 0
    my_feat = lax.axis_index("feat")
    core = my_feat & 1
    pieces = gather_half(residual)
    other_weight = exchange(enc_weight, "feat", 1)
    other_gate = exchange(jnp.stack([enc_bias, threshold]), "feat", 1)
    other_probe = exchange(probe_weight, "feat", 1)
    full_width = cols * feat_size
    square_sum = None
    for _, piece in pieces:
        values = piece.astype(jnp.float32)
        part = jnp.sum(values * values, axis=1)
        square_sum = part if square_sum is None else square_sum + part
    scale = lax.rsqrt(square_sum / full_width + epsilon)[:, None]
    preact = [None, None]
    for chip, piece in pieces:
        normed = (piece.astype(jnp.float32) * scale).astype(jnp.bfloat16)
        for g, weight in enumerate((enc_weight, other_weight)):
            weight_rows = lax.dynamic_slice_in_dim(weight, chip * 2 * cols, 2 * cols, 0)
            part = jnp.dot(normed, weight_rows, preferred_element_type=jnp.float32)
            preact[g] = part if preact[g] is None else preact[g] + part
    gates = ((enc_bias, threshold), (other_gate[0], other_gate[1]))
    features = []
    for g in range(2):
        encode_preact = preact[g] + gates[g][0]
        gate = jax.nn.sigmoid((encode_preact - gates[g][1]) / smooth_width)
        features.append((encode_preact * gate).astype(jnp.bfloat16))
    partial_value = jnp.dot(features[0], probe_weight, preferred_element_type=jnp.float32)
    partial_value = partial_value + jnp.dot(features[1], other_probe, preferred_element_type=jnp.float32)
    logits = reduce_sum(partial_value)
    classes = probe_weight.shape[1]
    class_ids = jnp.arange(classes, dtype=jnp.int32)
    my_labels = lax.dynamic_slice_in_dim(labels.reshape(tok_size, rows), core * half, half, 1).reshape(-1)
    softmax_logits = logits + probe_bias
    exps = jnp.exp(softmax_logits)
    totals = jnp.sum(exps, axis=1, keepdims=True)
    onehot = (my_labels[:, None] == class_ids[None, :]).astype(jnp.float32)
    losses = jnp.log(totals[:, 0]) - jnp.sum(onehot * softmax_logits, axis=1)
    delta = (exps / totals - onehot).astype(jnp.bfloat16)
    num_tokens = tok_size * rows
    share_rows = num_tokens // (feat_size * tok_size)
    start = lax.axis_index(("feat", "tok")) * share_rows
    token_loss = lax.dynamic_slice_in_dim(
        losses, (start // rows) * half + start % rows - core * half, share_rows, 0
    )
    gradient = jnp.dot(features[0].T, delta, preferred_element_type=jnp.float32)
    gradient_other = jnp.dot(features[1].T, delta, preferred_element_type=jnp.float32)
    gradient = gradient + exchange(gradient_other, "feat", 1)
    return (gradient, token_loss)


def solution(mesh):
    in_specs = (
        P("tok", "feat"),
        P(None, ("feat", "tok")),
        P(("feat", "tok")),
        P(("feat", "tok")),
        P(("feat", "tok"), None),
        P(),
        P(),
    )
    out_specs = (P(("feat", "tok"), None), P(("feat", "tok")))
    return jax.shard_map(local, mesh=mesh, in_specs=in_specs, out_specs=out_specs, check_vma=False)
```

```python
import jax
import jax.numpy as jnp
from jax import lax
from jax.sharding import PartitionSpec as P

epsilon = 1e-06
smooth_width = 0.125


def exchange(value, axis, offset):
    size = lax.axis_size(axis)
    return lax.ppermute(value, axis, [(i, i ^ offset) for i in range(size)])


def tok_partners():
    return list(range(1, lax.axis_size("tok")))


def chip_partners():
    return list(range(2, lax.axis_size("feat"), 2))


def ordered(bit_set, mine, got, axis):
    first = jnp.logical_not(bit_set)
    return jnp.concatenate([jnp.where(first, mine, got), jnp.where(first, got, mine)], axis=axis)


def tok_bits_of():
    return lax.axis_size("tok").bit_length() - 1


def reverse_bits(value, count):
    out = 0 * value
    for i in range(count):
        out = out + (((value >> i) & 1) << (count - 1 - i))
    return out


def gather_half(block):
    rows, cols = block.shape
    half = rows // 2
    my_tok = lax.axis_index("tok")
    my_feat = lax.axis_index("feat")
    core = my_feat & 1
    keep = lax.dynamic_slice_in_dim(block, core * half, half, 0)
    send = lax.dynamic_slice_in_dim(block, (1 - core) * half, half, 0)
    got = exchange(send, "feat", 1)
    held = ordered(core, keep, got, 1)
    for bit in reversed(range(tok_bits_of())):
        other = exchange(held, "tok", 1 << bit)
        held = ordered((my_tok >> bit) & 1, held, other, 0)
    my_chip = my_feat >> 1
    pieces = [(my_chip, held)]
    for k in chip_partners():
        pieces.append((my_chip ^ (k >> 1), exchange(held, "feat", k)))
    values = held.astype(jnp.float32)
    square_sum = jnp.sum(values * values, axis=1)
    total = square_sum
    for k in chip_partners():
        total = total + exchange(square_sum, "feat", k)
    full_width = cols * lax.axis_size("feat")
    scale = lax.rsqrt(total / full_width + epsilon)[:, None]
    return pieces, scale


def reduce_sum(value):
    total = value
    for k in tok_partners():
        total = total + exchange(value, "tok", k)
    value = total
    total = value
    for k in chip_partners():
        total = total + exchange(value, "feat", k)
    return total


def local(residual, enc_weight, enc_bias, threshold, probe_weight, probe_bias, labels):
    rows, cols = residual.shape
    half = rows // 2
    feat_size = lax.axis_size("feat")
    tok_size = lax.axis_size("tok")
    assert feat_size == 2 * tok_size and rows % 2 == 0
    my_feat = lax.axis_index("feat")
    core = my_feat & 1
    pieces, scale = gather_half(residual)
    other_weight = exchange(enc_weight, "feat", 1)
    other_gate = exchange(jnp.stack([enc_bias, threshold]), "feat", 1)
    other_probe = exchange(probe_weight, "feat", 1)
    preact = [None, None]
    for chip, piece in pieces:
        normed = (piece.astype(jnp.float32) * scale).astype(jnp.bfloat16)
        for g, weight in enumerate((enc_weight, other_weight)):
            weight_rows = lax.dynamic_slice_in_dim(weight, chip * 2 * cols, 2 * cols, 0)
            part = jnp.dot(normed, weight_rows, preferred_element_type=jnp.float32)
            preact[g] = part if preact[g] is None else preact[g] + part
    gates = ((enc_bias, threshold), (other_gate[0], other_gate[1]))
    features = []
    for g in range(2):
        encode_preact = preact[g] + gates[g][0]
        gate = jax.nn.sigmoid((encode_preact - gates[g][1]) / smooth_width)
        features.append((encode_preact * gate).astype(jnp.bfloat16))
    partial_value = jnp.dot(features[0], probe_weight, preferred_element_type=jnp.float32)
    partial_value = partial_value + jnp.dot(features[1], other_probe, preferred_element_type=jnp.float32)
    logits = reduce_sum(partial_value)
    classes = probe_weight.shape[1]
    class_ids = jnp.arange(classes, dtype=jnp.int32)
    bits = tok_bits_of()
    block_order = [reverse_bits(p, bits) for p in range(tok_size)]
    label_rows = labels.reshape(tok_size, rows)[jnp.array(block_order, jnp.int32)]
    my_labels = lax.dynamic_slice_in_dim(label_rows, core * half, half, 1).reshape(-1)
    softmax_logits = logits + probe_bias
    exps = jnp.exp(softmax_logits)
    totals = jnp.sum(exps, axis=1, keepdims=True)
    onehot = (my_labels[:, None] == class_ids[None, :]).astype(jnp.float32)
    losses = jnp.log(totals[:, 0]) - jnp.sum(onehot * softmax_logits, axis=1)
    delta = (exps / totals - onehot).astype(jnp.bfloat16)
    num_tokens = tok_size * rows
    share_rows = num_tokens // (feat_size * tok_size)
    start = lax.axis_index(("feat", "tok")) * share_rows
    token_loss = lax.dynamic_slice_in_dim(
        losses, reverse_bits(start // rows, bits) * half + start % rows - core * half, share_rows, 0
    )
    gradient = jnp.dot(features[0].T, delta, preferred_element_type=jnp.float32)
    gradient_other = jnp.dot(features[1].T, delta, preferred_element_type=jnp.float32)
    gradient = gradient + exchange(gradient_other, "feat", 1)
    return (gradient, token_loss)


def solution(mesh):
    in_specs = (
        P("tok", "feat"),
        P(None, ("feat", "tok")),
        P(("feat", "tok")),
        P(("feat", "tok")),
        P(("feat", "tok"), None),
        P(),
        P(),
    )
    out_specs = (P(("feat", "tok"), None), P(("feat", "tok")))
    return jax.shard_map(local, mesh=mesh, in_specs=in_specs, out_specs=out_specs, check_vma=False)
```

```python
import jax
import jax.numpy as jnp
from jax import lax
from jax.sharding import PartitionSpec as P

epsilon = 1e-06
smooth_width = 0.125


def exchange(value, axis, offset):
    size = lax.axis_size(axis)
    return lax.ppermute(value, axis, [(i, i ^ offset) for i in range(size)])


def tok_partners():
    return list(range(1, lax.axis_size("tok")))


def chip_partners():
    return list(range(2, lax.axis_size("feat"), 2))


def ordered(bit_set, mine, got, axis):
    first = jnp.logical_not(bit_set)
    return jnp.concatenate([jnp.where(first, mine, got), jnp.where(first, got, mine)], axis=axis)


def tok_bits_of():
    return lax.axis_size("tok").bit_length() - 1


def reverse_bits(value, count):
    out = 0 * value
    for i in range(count):
        out = out + (((value >> i) & 1) << (count - 1 - i))
    return out


def gather_half(block):
    rows, cols = block.shape
    half = rows // 2
    my_tok = lax.axis_index("tok")
    my_feat = lax.axis_index("feat")
    core = my_feat & 1
    keep = lax.dynamic_slice_in_dim(block, core * half, half, 0)
    send = lax.dynamic_slice_in_dim(block, (1 - core) * half, half, 0)
    got = exchange(send, "feat", 1)
    held = ordered(core, keep, got, 1)
    for bit in reversed(range(tok_bits_of())):
        other = exchange(held, "tok", 1 << bit)
        held = ordered((my_tok >> bit) & 1, held, other, 0)
    my_chip = my_feat >> 1
    pieces = [(my_chip, held)]
    for k in chip_partners():
        pieces.append((my_chip ^ (k >> 1), exchange(held, "feat", k)))
    return pieces


def reduce_sum(value):
    total = value
    for k in chip_partners():
        total = total + exchange(value, "feat", k)
    value = total
    total = value
    for k in tok_partners():
        total = total + exchange(value, "tok", k)
    return total


def local(residual, enc_weight, enc_bias, threshold, probe_weight, probe_bias, labels):
    rows, cols = residual.shape
    half = rows // 2
    feat_size = lax.axis_size("feat")
    tok_size = lax.axis_size("tok")
    assert feat_size == 2 * tok_size and rows % 2 == 0
    my_feat = lax.axis_index("feat")
    core = my_feat & 1
    pieces = gather_half(residual)
    other_weight = exchange(enc_weight, "feat", 1)
    other_gate = exchange(jnp.stack([enc_bias, threshold]), "feat", 1)
    other_probe = exchange(probe_weight, "feat", 1)
    full_width = cols * feat_size
    square_sum = None
    for _, piece in pieces:
        values = piece.astype(jnp.float32)
        part = jnp.sum(values * values, axis=1)
        square_sum = part if square_sum is None else square_sum + part
    scale = lax.rsqrt(square_sum / full_width + epsilon)[:, None]
    preact = [None, None]
    for chip, piece in pieces:
        normed = (piece.astype(jnp.float32) * scale).astype(jnp.bfloat16)
        for g, weight in enumerate((enc_weight, other_weight)):
            weight_rows = lax.dynamic_slice_in_dim(weight, chip * 2 * cols, 2 * cols, 0)
            part = jnp.dot(normed, weight_rows, preferred_element_type=jnp.float32)
            preact[g] = part if preact[g] is None else preact[g] + part
    gates = ((enc_bias, threshold), (other_gate[0], other_gate[1]))
    features = []
    for g in range(2):
        encode_preact = preact[g] + gates[g][0]
        gate = jax.nn.sigmoid((encode_preact - gates[g][1]) / smooth_width)
        features.append((encode_preact * gate).astype(jnp.bfloat16))
    partial_value = jnp.dot(features[0], probe_weight, preferred_element_type=jnp.float32)
    partial_value = partial_value + jnp.dot(features[1], other_probe, preferred_element_type=jnp.float32)
    logits = reduce_sum(partial_value)
    classes = probe_weight.shape[1]
    class_ids = jnp.arange(classes, dtype=jnp.int32)
    bits = tok_bits_of()
    block_order = [reverse_bits(p, bits) for p in range(tok_size)]
    label_rows = labels.reshape(tok_size, rows)[jnp.array(block_order, jnp.int32)]
    my_labels = lax.dynamic_slice_in_dim(label_rows, core * half, half, 1).reshape(-1)
    softmax_logits = logits + probe_bias
    exps = jnp.exp(softmax_logits)
    totals = jnp.sum(exps, axis=1, keepdims=True)
    onehot = (my_labels[:, None] == class_ids[None, :]).astype(jnp.float32)
    losses = jnp.log(totals[:, 0]) - jnp.sum(onehot * softmax_logits, axis=1)
    delta = (exps / totals - onehot).astype(jnp.bfloat16)
    num_tokens = tok_size * rows
    share_rows = num_tokens // (feat_size * tok_size)
    start = lax.axis_index(("feat", "tok")) * share_rows
    token_loss = lax.dynamic_slice_in_dim(
        losses, reverse_bits(start // rows, bits) * half + start % rows - core * half, share_rows, 0
    )
    gradient = jnp.dot(features[0].T, delta, preferred_element_type=jnp.float32)
    gradient_other = jnp.dot(features[1].T, delta, preferred_element_type=jnp.float32)
    gradient = gradient + exchange(gradient_other, "feat", 1)
    return (gradient, token_loss)


def solution(mesh):
    in_specs = (
        P("tok", "feat"),
        P(None, ("feat", "tok")),
        P(("feat", "tok")),
        P(("feat", "tok")),
        P(("feat", "tok"), None),
        P(),
        P(),
    )
    out_specs = (P(("feat", "tok"), None), P(("feat", "tok")))
    return jax.shard_map(local, mesh=mesh, in_specs=in_specs, out_specs=out_specs, check_vma=False)
```

```python
import jax
import jax.numpy as jnp
from jax import lax
from jax.sharding import PartitionSpec as P

epsilon = 1e-06
smooth_width = 0.125


def exchange(value, axis, offset):
    size = lax.axis_size(axis)
    return lax.ppermute(value, axis, [(i, i ^ offset) for i in range(size)])


def tok_partners():
    return list(range(1, lax.axis_size("tok")))


def chip_partners():
    return list(range(2, lax.axis_size("feat"), 2))


def ordered(bit_set, mine, got, axis):
    first = jnp.logical_not(bit_set)
    return jnp.concatenate([jnp.where(first, mine, got), jnp.where(first, got, mine)], axis=axis)


def tok_bits_of():
    return lax.axis_size("tok").bit_length() - 1


def reverse_bits(value, count):
    out = 0 * value
    for i in range(count):
        out = out + (((value >> i) & 1) << (count - 1 - i))
    return out


def gather_half(block):
    rows, cols = block.shape
    half = rows // 2
    my_tok = lax.axis_index("tok")
    my_feat = lax.axis_index("feat")
    core = my_feat & 1
    got = exchange(block, "feat", 1)
    keep = lax.dynamic_slice_in_dim(block, core * half, half, 0)
    theirs = lax.dynamic_slice_in_dim(got, core * half, half, 0)
    held = ordered(core, keep, theirs, 1)
    for bit in reversed(range(tok_bits_of())):
        other = exchange(held, "tok", 1 << bit)
        held = ordered((my_tok >> bit) & 1, held, other, 0)
    my_chip = my_feat >> 1
    pieces = [(my_chip, held)]
    for k in chip_partners():
        pieces.append((my_chip ^ (k >> 1), exchange(held, "feat", k)))
    return pieces


def reduce_sum(value):
    total = value
    for k in tok_partners():
        total = total + exchange(value, "tok", k)
    value = total
    total = value
    for k in chip_partners():
        total = total + exchange(value, "feat", k)
    return total


def local(residual, enc_weight, enc_bias, threshold, probe_weight, probe_bias, labels):
    rows, cols = residual.shape
    half = rows // 2
    feat_size = lax.axis_size("feat")
    tok_size = lax.axis_size("tok")
    assert feat_size == 2 * tok_size and rows % 2 == 0
    my_feat = lax.axis_index("feat")
    core = my_feat & 1
    pieces = gather_half(residual)
    other_weight = exchange(enc_weight, "feat", 1)
    other_gate = exchange(jnp.stack([enc_bias, threshold]), "feat", 1)
    other_probe = exchange(probe_weight, "feat", 1)
    full_width = cols * feat_size
    square_sum = None
    for _, piece in pieces:
        values = piece.astype(jnp.float32)
        part = jnp.sum(values * values, axis=1)
        square_sum = part if square_sum is None else square_sum + part
    scale = lax.rsqrt(square_sum / full_width + epsilon)[:, None]
    preact = [None, None]
    for chip, piece in pieces:
        normed = (piece.astype(jnp.float32) * scale).astype(jnp.bfloat16)
        for g, weight in enumerate((enc_weight, other_weight)):
            weight_rows = lax.dynamic_slice_in_dim(weight, chip * 2 * cols, 2 * cols, 0)
            part = jnp.dot(normed, weight_rows, preferred_element_type=jnp.float32)
            preact[g] = part if preact[g] is None else preact[g] + part
    gates = ((enc_bias, threshold), (other_gate[0], other_gate[1]))
    features = []
    for g in range(2):
        encode_preact = preact[g] + gates[g][0]
        gate = jax.nn.sigmoid((encode_preact - gates[g][1]) / smooth_width)
        features.append((encode_preact * gate).astype(jnp.bfloat16))
    partial_value = jnp.dot(features[0], probe_weight, preferred_element_type=jnp.float32)
    partial_value = partial_value + jnp.dot(features[1], other_probe, preferred_element_type=jnp.float32)
    logits = reduce_sum(partial_value)
    classes = probe_weight.shape[1]
    class_ids = jnp.arange(classes, dtype=jnp.int32)
    bits = tok_bits_of()
    block_order = [reverse_bits(p, bits) for p in range(tok_size)]
    label_rows = labels.reshape(tok_size, rows)[jnp.array(block_order, jnp.int32)]
    my_labels = lax.dynamic_slice_in_dim(label_rows, core * half, half, 1).reshape(-1)
    softmax_logits = logits + probe_bias
    exps = jnp.exp(softmax_logits)
    totals = jnp.sum(exps, axis=1, keepdims=True)
    onehot = (my_labels[:, None] == class_ids[None, :]).astype(jnp.float32)
    losses = jnp.log(totals[:, 0]) - jnp.sum(onehot * softmax_logits, axis=1)
    delta = (exps / totals - onehot).astype(jnp.bfloat16)
    num_tokens = tok_size * rows
    share_rows = num_tokens // (feat_size * tok_size)
    start = lax.axis_index(("feat", "tok")) * share_rows
    token_loss = lax.dynamic_slice_in_dim(
        losses, reverse_bits(start // rows, bits) * half + start % rows - core * half, share_rows, 0
    )
    gradient = jnp.dot(features[0].T, delta, preferred_element_type=jnp.float32)
    gradient_other = jnp.dot(features[1].T, delta, preferred_element_type=jnp.float32)
    gradient = gradient + exchange(gradient_other, "feat", 1)
    return (gradient, token_loss)


def solution(mesh):
    in_specs = (
        P("tok", "feat"),
        P(None, ("feat", "tok")),
        P(("feat", "tok")),
        P(("feat", "tok")),
        P(("feat", "tok"), None),
        P(),
        P(),
    )
    out_specs = (P(("feat", "tok"), None), P(("feat", "tok")))
    return jax.shard_map(local, mesh=mesh, in_specs=in_specs, out_specs=out_specs, check_vma=False)
```

```python
import jax
import jax.numpy as jnp
from jax import lax
from jax.sharding import PartitionSpec as P

epsilon = 1e-06
smooth_width = 0.125


def exchange(value, axis, offset):
    size = lax.axis_size(axis)
    return lax.ppermute(value, axis, [(i, i ^ offset) for i in range(size)])


def tok_partners():
    return list(range(1, lax.axis_size("tok")))


def chip_partners():
    return list(range(2, lax.axis_size("feat"), 2))


def ordered(bit_set, mine, got, axis):
    first = jnp.logical_not(bit_set)
    return jnp.concatenate([jnp.where(first, mine, got), jnp.where(first, got, mine)], axis=axis)


def tok_bits_of():
    return lax.axis_size("tok").bit_length() - 1


def reverse_bits(value, count):
    out = 0 * value
    for i in range(count):
        out = out + (((value >> i) & 1) << (count - 1 - i))
    return out


def gather_half(block):
    rows, cols = block.shape
    half = rows // 2
    my_tok = lax.axis_index("tok")
    my_feat = lax.axis_index("feat")
    core = my_feat & 1
    got = exchange(block, "feat", 1)
    keep = lax.dynamic_slice_in_dim(block, core * half, half, 0)
    theirs = lax.dynamic_slice_in_dim(got, core * half, half, 0)
    held = ordered(core, keep, theirs, 1)
    for bit in reversed(range(tok_bits_of())):
        other = exchange(held, "tok", 1 << bit)
        held = ordered((my_tok >> bit) & 1, held, other, 0)
    my_chip = my_feat >> 1
    pieces = [(my_chip, held)]
    for k in chip_partners():
        pieces.append((my_chip ^ (k >> 1), exchange(held, "feat", k)))
    return pieces


def reduce_sum(value):
    total = value
    for k in tok_partners():
        total = total + exchange(value, "tok", k)
    value = total
    total = value
    for k in chip_partners():
        total = total + exchange(value, "feat", k)
    return total


def local(residual, enc_weight, enc_bias, threshold, probe_weight, probe_bias, labels):
    rows, cols = residual.shape
    half = rows // 2
    feat_size = lax.axis_size("feat")
    tok_size = lax.axis_size("tok")
    assert feat_size == 2 * tok_size and rows % 2 == 0
    my_feat = lax.axis_index("feat")
    core = my_feat & 1
    pieces = gather_half(residual)
    other_weight = exchange(enc_weight, "feat", 1)
    other_gate = exchange(jnp.stack([enc_bias, threshold]), "feat", 1)
    other_probe = exchange(probe_weight, "feat", 1)
    full_width = cols * feat_size
    square_sum = None
    for _, piece in pieces:
        values = piece.astype(jnp.float32)
        part = jnp.sum(values * values, axis=1)
        square_sum = part if square_sum is None else square_sum + part
    scale = lax.rsqrt(square_sum / full_width + epsilon)[:, None]
    whole = jnp.zeros((pieces[0][1].shape[0], full_width), residual.dtype)
    for chip, piece in pieces:
        whole = lax.dynamic_update_slice(whole, piece, (0, chip * 2 * cols))
    normed = (whole.astype(jnp.float32) * scale).astype(jnp.bfloat16)
    preact = [
        jnp.dot(normed, weight, preferred_element_type=jnp.float32)
        for weight in (enc_weight, other_weight)
    ]
    gates = ((enc_bias, threshold), (other_gate[0], other_gate[1]))
    features = []
    for g in range(2):
        encode_preact = preact[g] + gates[g][0]
        gate = jax.nn.sigmoid((encode_preact - gates[g][1]) / smooth_width)
        features.append((encode_preact * gate).astype(jnp.bfloat16))
    partial_value = jnp.dot(features[0], probe_weight, preferred_element_type=jnp.float32)
    partial_value = partial_value + jnp.dot(features[1], other_probe, preferred_element_type=jnp.float32)
    logits = reduce_sum(partial_value)
    classes = probe_weight.shape[1]
    class_ids = jnp.arange(classes, dtype=jnp.int32)
    bits = tok_bits_of()
    block_order = [reverse_bits(p, bits) for p in range(tok_size)]
    label_rows = labels.reshape(tok_size, rows)[jnp.array(block_order, jnp.int32)]
    my_labels = lax.dynamic_slice_in_dim(label_rows, core * half, half, 1).reshape(-1)
    softmax_logits = logits + probe_bias
    exps = jnp.exp(softmax_logits)
    totals = jnp.sum(exps, axis=1, keepdims=True)
    onehot = (my_labels[:, None] == class_ids[None, :]).astype(jnp.float32)
    losses = jnp.log(totals[:, 0]) - jnp.sum(onehot * softmax_logits, axis=1)
    delta = (exps / totals - onehot).astype(jnp.bfloat16)
    num_tokens = tok_size * rows
    share_rows = num_tokens // (feat_size * tok_size)
    start = lax.axis_index(("feat", "tok")) * share_rows
    token_loss = lax.dynamic_slice_in_dim(
        losses, reverse_bits(start // rows, bits) * half + start % rows - core * half, share_rows, 0
    )
    gradient = jnp.dot(features[0].T, delta, preferred_element_type=jnp.float32)
    gradient_other = jnp.dot(features[1].T, delta, preferred_element_type=jnp.float32)
    gradient = gradient + exchange(gradient_other, "feat", 1)
    return (gradient, token_loss)


def solution(mesh):
    in_specs = (
        P("tok", "feat"),
        P(None, ("feat", "tok")),
        P(("feat", "tok")),
        P(("feat", "tok")),
        P(("feat", "tok"), None),
        P(),
        P(),
    )
    out_specs = (P(("feat", "tok"), None), P(("feat", "tok")))
    return jax.shard_map(local, mesh=mesh, in_specs=in_specs, out_specs=out_specs, check_vma=False)
```

```python
import jax
import jax.numpy as jnp
from jax import lax
from jax.sharding import PartitionSpec as P

epsilon = 1e-06
smooth_width = 0.125


def exchange(value, axis, offset):
    size = lax.axis_size(axis)
    return lax.ppermute(value, axis, [(i, i ^ offset) for i in range(size)])


def tok_partners():
    return list(range(1, lax.axis_size("tok")))


def chip_partners():
    return list(range(2, lax.axis_size("feat"), 2))


def ordered(bit_set, mine, got, axis):
    first = jnp.logical_not(bit_set)
    return jnp.concatenate([jnp.where(first, mine, got), jnp.where(first, got, mine)], axis=axis)


def tok_bits_of():
    return lax.axis_size("tok").bit_length() - 1


def reverse_bits(value, count):
    out = 0 * value
    for i in range(count):
        out = out + (((value >> i) & 1) << (count - 1 - i))
    return out


def gather_half(block):
    rows, cols = block.shape
    half = rows // 2
    my_tok = lax.axis_index("tok")
    my_feat = lax.axis_index("feat")
    core = my_feat & 1
    got = exchange(block, "feat", 1)
    keep = lax.dynamic_slice_in_dim(block, core * half, half, 0)
    theirs = lax.dynamic_slice_in_dim(got, core * half, half, 0)
    held = ordered(core, keep, theirs, 1)
    for bit in reversed(range(tok_bits_of())):
        other = exchange(held, "tok", 1 << bit)
        held = ordered((my_tok >> bit) & 1, held, other, 0)
    my_chip = my_feat >> 1
    pieces = [(my_chip, held)]
    for k in chip_partners():
        pieces.append((my_chip ^ (k >> 1), exchange(held, "feat", k)))
    return pieces


def reduce_sum(value):
    total = value
    for k in tok_partners():
        total = total + exchange(value, "tok", k)
    value = total
    total = value
    for k in chip_partners():
        total = total + exchange(value, "feat", k)
    return total


def local(residual, enc_weight, enc_bias, threshold, probe_weight, probe_bias, labels):
    rows, cols = residual.shape
    half = rows // 2
    feat_size = lax.axis_size("feat")
    tok_size = lax.axis_size("tok")
    assert feat_size == 2 * tok_size and rows % 2 == 0
    my_feat = lax.axis_index("feat")
    core = my_feat & 1
    pieces = gather_half(residual)
    other_weight = exchange(enc_weight, "feat", 1)
    other_gate = exchange(jnp.stack([enc_bias, threshold]), "feat", 1)
    other_probe = exchange(probe_weight, "feat", 1)
    full_width = cols * feat_size
    square_sum = None
    for _, piece in pieces:
        values = piece.astype(jnp.float32)
        part = jnp.sum(values * values, axis=1)
        square_sum = part if square_sum is None else square_sum + part
    scale = lax.rsqrt(square_sum / full_width + epsilon)[:, None]
    whole = jnp.zeros((pieces[0][1].shape[0], full_width), residual.dtype)
    for chip, piece in pieces:
        whole = lax.dynamic_update_slice(whole, piece, (0, chip * 2 * cols))
    normed = lax.optimization_barrier((whole.astype(jnp.float32) * scale).astype(jnp.bfloat16))
    preact = [
        jnp.dot(normed, weight, preferred_element_type=jnp.float32)
        for weight in (enc_weight, other_weight)
    ]
    gates = ((enc_bias, threshold), (other_gate[0], other_gate[1]))
    features = []
    for g in range(2):
        encode_preact = preact[g] + gates[g][0]
        gate = jax.nn.sigmoid((encode_preact - gates[g][1]) / smooth_width)
        features.append((encode_preact * gate).astype(jnp.bfloat16))
    partial_value = jnp.dot(features[0], probe_weight, preferred_element_type=jnp.float32)
    partial_value = partial_value + jnp.dot(features[1], other_probe, preferred_element_type=jnp.float32)
    logits = reduce_sum(partial_value)
    classes = probe_weight.shape[1]
    class_ids = jnp.arange(classes, dtype=jnp.int32)
    bits = tok_bits_of()
    block_order = [reverse_bits(p, bits) for p in range(tok_size)]
    label_rows = labels.reshape(tok_size, rows)[jnp.array(block_order, jnp.int32)]
    my_labels = lax.dynamic_slice_in_dim(label_rows, core * half, half, 1).reshape(-1)
    softmax_logits = logits + probe_bias
    exps = jnp.exp(softmax_logits)
    totals = jnp.sum(exps, axis=1, keepdims=True)
    onehot = (my_labels[:, None] == class_ids[None, :]).astype(jnp.float32)
    losses = jnp.log(totals[:, 0]) - jnp.sum(onehot * softmax_logits, axis=1)
    delta = (exps / totals - onehot).astype(jnp.bfloat16)
    num_tokens = tok_size * rows
    share_rows = num_tokens // (feat_size * tok_size)
    start = lax.axis_index(("feat", "tok")) * share_rows
    token_loss = lax.dynamic_slice_in_dim(
        losses, reverse_bits(start // rows, bits) * half + start % rows - core * half, share_rows, 0
    )
    gradient = jnp.dot(features[0].T, delta, preferred_element_type=jnp.float32)
    gradient_other = jnp.dot(features[1].T, delta, preferred_element_type=jnp.float32)
    gradient = gradient + exchange(gradient_other, "feat", 1)
    return (gradient, token_loss)


def solution(mesh):
    in_specs = (
        P("tok", "feat"),
        P(None, ("feat", "tok")),
        P(("feat", "tok")),
        P(("feat", "tok")),
        P(("feat", "tok"), None),
        P(),
        P(),
    )
    out_specs = (P(("feat", "tok"), None), P(("feat", "tok")))
    return jax.shard_map(local, mesh=mesh, in_specs=in_specs, out_specs=out_specs, check_vma=False)
```

```python
import jax
import jax.numpy as jnp
from jax import lax
from jax.sharding import PartitionSpec as P

epsilon = 1e-06
smooth_width = 0.125


def exchange(value, axis, offset):
    size = lax.axis_size(axis)
    return lax.ppermute(value, axis, [(i, i ^ offset) for i in range(size)])


def tok_partners():
    return list(range(1, lax.axis_size("tok")))


def chip_partners():
    return list(range(2, lax.axis_size("feat"), 2))


def ordered(bit_set, mine, got, axis):
    first = jnp.logical_not(bit_set)
    return jnp.concatenate([jnp.where(first, mine, got), jnp.where(first, got, mine)], axis=axis)


def tok_bits_of():
    return lax.axis_size("tok").bit_length() - 1


def reverse_bits(value, count):
    out = 0 * value
    for i in range(count):
        out = out + (((value >> i) & 1) << (count - 1 - i))
    return out


def gather_half(block):
    rows, cols = block.shape
    half = rows // 2
    my_tok = lax.axis_index("tok")
    my_feat = lax.axis_index("feat")
    core = my_feat & 1
    got = exchange(block, "feat", 1)
    keep = lax.dynamic_slice_in_dim(block, core * half, half, 0)
    theirs = lax.dynamic_slice_in_dim(got, core * half, half, 0)
    held = ordered(core, keep, theirs, 1)
    for bit in reversed(range(tok_bits_of())):
        other = exchange(held, "tok", 1 << bit)
        held = ordered((my_tok >> bit) & 1, held, other, 0)
    my_chip = my_feat >> 1
    pieces = [(my_chip, held)]
    for k in chip_partners():
        pieces.append((my_chip ^ (k >> 1), exchange(held, "feat", k)))
    return pieces


def reduce_sum(value):
    total = value
    for k in tok_partners():
        total = total + exchange(value, "tok", k)
    value = total
    total = value
    for k in chip_partners():
        total = total + exchange(value, "feat", k)
    return total


def local(residual, enc_weight, enc_bias, threshold, probe_weight, probe_bias, labels):
    rows, cols = residual.shape
    half = rows // 2
    feat_size = lax.axis_size("feat")
    tok_size = lax.axis_size("tok")
    assert feat_size == 2 * tok_size and rows % 2 == 0
    my_feat = lax.axis_index("feat")
    core = my_feat & 1
    pieces = gather_half(residual)
    other_weight = exchange(enc_weight, "feat", 1)
    other_gate = exchange(jnp.stack([enc_bias, threshold]), "feat", 1)
    other_probe = exchange(probe_weight, "feat", 1)
    full_width = cols * feat_size
    square_sum = None
    for _, piece in pieces:
        values = piece.astype(jnp.float32)
        part = jnp.sum(values * values, axis=1)
        square_sum = part if square_sum is None else square_sum + part
    scale = lax.rsqrt(square_sum / full_width + epsilon)[:, None]
    whole = jnp.zeros((pieces[0][1].shape[0], full_width), residual.dtype)
    for chip, piece in pieces:
        whole = lax.dynamic_update_slice(whole, piece, (0, chip * 2 * cols))
    normed = (whole.astype(jnp.float32) * scale).astype(jnp.bfloat16)
    preact = [jnp.dot(normed, enc_weight, preferred_element_type=jnp.float32), None]
    for chip, piece in pieces:
        piece_normed = (piece.astype(jnp.float32) * scale).astype(jnp.bfloat16)
        weight_rows = lax.dynamic_slice_in_dim(other_weight, chip * 2 * cols, 2 * cols, 0)
        part = jnp.dot(piece_normed, weight_rows, preferred_element_type=jnp.float32)
        preact[1] = part if preact[1] is None else preact[1] + part
    gates = ((enc_bias, threshold), (other_gate[0], other_gate[1]))
    features = []
    for g in range(2):
        encode_preact = preact[g] + gates[g][0]
        gate = jax.nn.sigmoid((encode_preact - gates[g][1]) / smooth_width)
        features.append((encode_preact * gate).astype(jnp.bfloat16))
    partial_value = jnp.dot(features[0], probe_weight, preferred_element_type=jnp.float32)
    partial_value = partial_value + jnp.dot(features[1], other_probe, preferred_element_type=jnp.float32)
    logits = reduce_sum(partial_value)
    classes = probe_weight.shape[1]
    class_ids = jnp.arange(classes, dtype=jnp.int32)
    bits = tok_bits_of()
    block_order = [reverse_bits(p, bits) for p in range(tok_size)]
    label_rows = labels.reshape(tok_size, rows)[jnp.array(block_order, jnp.int32)]
    my_labels = lax.dynamic_slice_in_dim(label_rows, core * half, half, 1).reshape(-1)
    softmax_logits = logits + probe_bias
    exps = jnp.exp(softmax_logits)
    totals = jnp.sum(exps, axis=1, keepdims=True)
    onehot = (my_labels[:, None] == class_ids[None, :]).astype(jnp.float32)
    losses = jnp.log(totals[:, 0]) - jnp.sum(onehot * softmax_logits, axis=1)
    delta = (exps / totals - onehot).astype(jnp.bfloat16)
    num_tokens = tok_size * rows
    share_rows = num_tokens // (feat_size * tok_size)
    start = lax.axis_index(("feat", "tok")) * share_rows
    token_loss = lax.dynamic_slice_in_dim(
        losses, reverse_bits(start // rows, bits) * half + start % rows - core * half, share_rows, 0
    )
    gradient = jnp.dot(features[0].T, delta, preferred_element_type=jnp.float32)
    gradient_other = jnp.dot(features[1].T, delta, preferred_element_type=jnp.float32)
    gradient = gradient + exchange(gradient_other, "feat", 1)
    return (gradient, token_loss)


def solution(mesh):
    in_specs = (
        P("tok", "feat"),
        P(None, ("feat", "tok")),
        P(("feat", "tok")),
        P(("feat", "tok")),
        P(("feat", "tok"), None),
        P(),
        P(),
    )
    out_specs = (P(("feat", "tok"), None), P(("feat", "tok")))
    return jax.shard_map(local, mesh=mesh, in_specs=in_specs, out_specs=out_specs, check_vma=False)
```

```python
import jax
import jax.numpy as jnp
from jax import lax
from jax.sharding import PartitionSpec as P

epsilon = 1e-06
smooth_width = 0.125


def exchange(value, axis, offset):
    size = lax.axis_size(axis)
    return lax.ppermute(value, axis, [(i, i ^ offset) for i in range(size)])


def tok_partners():
    return list(range(1, lax.axis_size("tok")))


def chip_partners():
    return list(range(2, lax.axis_size("feat"), 2))


def ordered(bit_set, mine, got, axis):
    first = jnp.logical_not(bit_set)
    return jnp.concatenate([jnp.where(first, mine, got), jnp.where(first, got, mine)], axis=axis)


def tok_bits_of():
    return lax.axis_size("tok").bit_length() - 1


def reverse_bits(value, count):
    out = 0 * value
    for i in range(count):
        out = out + (((value >> i) & 1) << (count - 1 - i))
    return out


def gather_half(block):
    rows, cols = block.shape
    half = rows // 2
    my_tok = lax.axis_index("tok")
    my_feat = lax.axis_index("feat")
    core = my_feat & 1
    got = exchange(block, "feat", 1)
    keep = lax.dynamic_slice_in_dim(block, core * half, half, 0)
    theirs = lax.dynamic_slice_in_dim(got, core * half, half, 0)
    held = ordered(core, keep, theirs, 1)
    for bit in reversed(range(tok_bits_of())):
        other = exchange(held, "tok", 1 << bit)
        held = ordered((my_tok >> bit) & 1, held, other, 0)
    my_chip = my_feat >> 1
    pieces = [(my_chip, held)]
    for k in chip_partners():
        pieces.append((my_chip ^ (k >> 1), exchange(held, "feat", k)))
    return pieces


def reduce_sum(value):
    total = value
    for k in tok_partners():
        total = total + exchange(value, "tok", k)
    value = total
    total = value
    for k in chip_partners():
        total = total + exchange(value, "feat", k)
    return total


def local(residual, enc_weight, enc_bias, threshold, probe_weight, probe_bias, labels):
    rows, cols = residual.shape
    half = rows // 2
    feat_size = lax.axis_size("feat")
    tok_size = lax.axis_size("tok")
    assert feat_size == 2 * tok_size and rows % 2 == 0
    my_feat = lax.axis_index("feat")
    core = my_feat & 1
    pieces = gather_half(residual)
    other_weight = exchange(enc_weight, "feat", 1)
    other_gate = exchange(jnp.stack([enc_bias, threshold]), "feat", 1)
    other_probe = exchange(probe_weight, "feat", 1)
    full_width = cols * feat_size
    square_sum = None
    for _, piece in pieces:
        values = piece.astype(jnp.float32)
        part = jnp.sum(values * values, axis=1)
        square_sum = part if square_sum is None else square_sum + part
    scale = lax.rsqrt(square_sum / full_width + epsilon)[:, None]
    whole = jnp.zeros((pieces[0][1].shape[0], full_width), residual.dtype)
    for chip, piece in pieces:
        whole = lax.dynamic_update_slice(whole, piece, (0, chip * 2 * cols))
    normed = (whole.astype(jnp.float32) * scale).astype(jnp.bfloat16)
    width = enc_weight.shape[1]
    weight_both = jnp.concatenate([enc_weight, other_weight], axis=1)
    preact_both = jnp.dot(normed, weight_both, preferred_element_type=jnp.float32)
    preact = [preact_both[:, :width], preact_both[:, width:]]
    gates = ((enc_bias, threshold), (other_gate[0], other_gate[1]))
    features = []
    for g in range(2):
        encode_preact = preact[g] + gates[g][0]
        gate = jax.nn.sigmoid((encode_preact - gates[g][1]) / smooth_width)
        features.append((encode_preact * gate).astype(jnp.bfloat16))
    partial_value = jnp.dot(features[0], probe_weight, preferred_element_type=jnp.float32)
    partial_value = partial_value + jnp.dot(features[1], other_probe, preferred_element_type=jnp.float32)
    logits = reduce_sum(partial_value)
    classes = probe_weight.shape[1]
    class_ids = jnp.arange(classes, dtype=jnp.int32)
    bits = tok_bits_of()
    block_order = [reverse_bits(p, bits) for p in range(tok_size)]
    label_rows = labels.reshape(tok_size, rows)[jnp.array(block_order, jnp.int32)]
    my_labels = lax.dynamic_slice_in_dim(label_rows, core * half, half, 1).reshape(-1)
    softmax_logits = logits + probe_bias
    exps = jnp.exp(softmax_logits)
    totals = jnp.sum(exps, axis=1, keepdims=True)
    onehot = (my_labels[:, None] == class_ids[None, :]).astype(jnp.float32)
    losses = jnp.log(totals[:, 0]) - jnp.sum(onehot * softmax_logits, axis=1)
    delta = (exps / totals - onehot).astype(jnp.bfloat16)
    num_tokens = tok_size * rows
    share_rows = num_tokens // (feat_size * tok_size)
    start = lax.axis_index(("feat", "tok")) * share_rows
    token_loss = lax.dynamic_slice_in_dim(
        losses, reverse_bits(start // rows, bits) * half + start % rows - core * half, share_rows, 0
    )
    gradient = jnp.dot(features[0].T, delta, preferred_element_type=jnp.float32)
    gradient_other = jnp.dot(features[1].T, delta, preferred_element_type=jnp.float32)
    gradient = gradient + exchange(gradient_other, "feat", 1)
    return (gradient, token_loss)


def solution(mesh):
    in_specs = (
        P("tok", "feat"),
        P(None, ("feat", "tok")),
        P(("feat", "tok")),
        P(("feat", "tok")),
        P(("feat", "tok"), None),
        P(),
        P(),
    )
    out_specs = (P(("feat", "tok"), None), P(("feat", "tok")))
    return jax.shard_map(local, mesh=mesh, in_specs=in_specs, out_specs=out_specs, check_vma=False)
```

```python
import jax
import jax.numpy as jnp
from jax import lax
from jax.sharding import PartitionSpec as P

epsilon = 1e-06
smooth_width = 0.125


def exchange(value, axis, offset):
    size = lax.axis_size(axis)
    return lax.ppermute(value, axis, [(i, i ^ offset) for i in range(size)])


def tok_partners():
    return list(range(1, lax.axis_size("tok")))


def chip_partners():
    return list(reversed(range(2, lax.axis_size("feat"), 2)))


def ordered(bit_set, mine, got, axis):
    first = jnp.logical_not(bit_set)
    return jnp.concatenate([jnp.where(first, mine, got), jnp.where(first, got, mine)], axis=axis)


def tok_bits_of():
    return lax.axis_size("tok").bit_length() - 1


def reverse_bits(value, count):
    out = 0 * value
    for i in range(count):
        out = out + (((value >> i) & 1) << (count - 1 - i))
    return out


def gather_half(block):
    rows, cols = block.shape
    half = rows // 2
    my_tok = lax.axis_index("tok")
    my_feat = lax.axis_index("feat")
    core = my_feat & 1
    got = exchange(block, "feat", 1)
    keep = lax.dynamic_slice_in_dim(block, core * half, half, 0)
    theirs = lax.dynamic_slice_in_dim(got, core * half, half, 0)
    held = ordered(core, keep, theirs, 1)
    for bit in reversed(range(tok_bits_of())):
        other = exchange(held, "tok", 1 << bit)
        held = ordered((my_tok >> bit) & 1, held, other, 0)
    my_chip = my_feat >> 1
    pieces = [(my_chip, held)]
    for k in chip_partners():
        pieces.append((my_chip ^ (k >> 1), exchange(held, "feat", k)))
    return pieces


def reduce_sum(value):
    total = value
    for k in tok_partners():
        total = total + exchange(value, "tok", k)
    value = total
    total = value
    for k in chip_partners():
        total = total + exchange(value, "feat", k)
    return total


def local(residual, enc_weight, enc_bias, threshold, probe_weight, probe_bias, labels):
    rows, cols = residual.shape
    half = rows // 2
    feat_size = lax.axis_size("feat")
    tok_size = lax.axis_size("tok")
    assert feat_size == 2 * tok_size and rows % 2 == 0
    my_feat = lax.axis_index("feat")
    core = my_feat & 1
    pieces = gather_half(residual)
    other_weight = exchange(enc_weight, "feat", 1)
    other_gate = exchange(jnp.stack([enc_bias, threshold]), "feat", 1)
    other_probe = exchange(probe_weight, "feat", 1)
    full_width = cols * feat_size
    square_sum = None
    for _, piece in pieces:
        values = piece.astype(jnp.float32)
        part = jnp.sum(values * values, axis=1)
        square_sum = part if square_sum is None else square_sum + part
    scale = lax.rsqrt(square_sum / full_width + epsilon)[:, None]
    whole = jnp.zeros((pieces[0][1].shape[0], full_width), residual.dtype)
    for chip, piece in pieces:
        whole = lax.dynamic_update_slice(whole, piece, (0, chip * 2 * cols))
    normed = (whole.astype(jnp.float32) * scale).astype(jnp.bfloat16)
    preact = [
        jnp.dot(normed, weight, preferred_element_type=jnp.float32)
        for weight in (enc_weight, other_weight)
    ]
    gates = ((enc_bias, threshold), (other_gate[0], other_gate[1]))
    features = []
    for g in range(2):
        encode_preact = preact[g] + gates[g][0]
        gate = jax.nn.sigmoid((encode_preact - gates[g][1]) / smooth_width)
        features.append((encode_preact * gate).astype(jnp.bfloat16))
    partial_value = jnp.dot(features[0], probe_weight, preferred_element_type=jnp.float32)
    partial_value = partial_value + jnp.dot(features[1], other_probe, preferred_element_type=jnp.float32)
    logits = reduce_sum(partial_value)
    classes = probe_weight.shape[1]
    class_ids = jnp.arange(classes, dtype=jnp.int32)
    bits = tok_bits_of()
    block_order = [reverse_bits(p, bits) for p in range(tok_size)]
    label_rows = labels.reshape(tok_size, rows)[jnp.array(block_order, jnp.int32)]
    my_labels = lax.dynamic_slice_in_dim(label_rows, core * half, half, 1).reshape(-1)
    softmax_logits = logits + probe_bias
    exps = jnp.exp(softmax_logits)
    totals = jnp.sum(exps, axis=1, keepdims=True)
    onehot = (my_labels[:, None] == class_ids[None, :]).astype(jnp.float32)
    losses = jnp.log(totals[:, 0]) - jnp.sum(onehot * softmax_logits, axis=1)
    delta = (exps / totals - onehot).astype(jnp.bfloat16)
    num_tokens = tok_size * rows
    share_rows = num_tokens // (feat_size * tok_size)
    start = lax.axis_index(("feat", "tok")) * share_rows
    token_loss = lax.dynamic_slice_in_dim(
        losses, reverse_bits(start // rows, bits) * half + start % rows - core * half, share_rows, 0
    )
    gradient = jnp.dot(features[0].T, delta, preferred_element_type=jnp.float32)
    gradient_other = jnp.dot(features[1].T, delta, preferred_element_type=jnp.float32)
    gradient = gradient + exchange(gradient_other, "feat", 1)
    return (gradient, token_loss)


def solution(mesh):
    in_specs = (
        P("tok", "feat"),
        P(None, ("feat", "tok")),
        P(("feat", "tok")),
        P(("feat", "tok")),
        P(("feat", "tok"), None),
        P(),
        P(),
    )
    out_specs = (P(("feat", "tok"), None), P(("feat", "tok")))
    return jax.shard_map(local, mesh=mesh, in_specs=in_specs, out_specs=out_specs, check_vma=False)
```

```python
import jax
import jax.numpy as jnp
from jax import lax
from jax.sharding import PartitionSpec as P

epsilon = 1e-06
smooth_width = 0.125


def exchange(value, axis, offset):
    size = lax.axis_size(axis)
    return lax.ppermute(value, axis, [(i, i ^ offset) for i in range(size)])


def tok_partners():
    return list(reversed(range(1, lax.axis_size("tok"))))


def chip_partners():
    return list(range(2, lax.axis_size("feat"), 2))


def ordered(bit_set, mine, got, axis):
    first = jnp.logical_not(bit_set)
    return jnp.concatenate([jnp.where(first, mine, got), jnp.where(first, got, mine)], axis=axis)


def tok_bits_of():
    return lax.axis_size("tok").bit_length() - 1


def reverse_bits(value, count):
    out = 0 * value
    for i in range(count):
        out = out + (((value >> i) & 1) << (count - 1 - i))
    return out


def gather_half(block):
    rows, cols = block.shape
    half = rows // 2
    my_tok = lax.axis_index("tok")
    my_feat = lax.axis_index("feat")
    core = my_feat & 1
    got = exchange(block, "feat", 1)
    keep = lax.dynamic_slice_in_dim(block, core * half, half, 0)
    theirs = lax.dynamic_slice_in_dim(got, core * half, half, 0)
    held = ordered(core, keep, theirs, 1)
    for bit in reversed(range(tok_bits_of())):
        other = exchange(held, "tok", 1 << bit)
        held = ordered((my_tok >> bit) & 1, held, other, 0)
    my_chip = my_feat >> 1
    pieces = [(my_chip, held)]
    for k in chip_partners():
        pieces.append((my_chip ^ (k >> 1), exchange(held, "feat", k)))
    return pieces


def reduce_sum(value):
    total = value
    for k in tok_partners():
        total = total + exchange(value, "tok", k)
    value = total
    total = value
    for k in chip_partners():
        total = total + exchange(value, "feat", k)
    return total


def local(residual, enc_weight, enc_bias, threshold, probe_weight, probe_bias, labels):
    rows, cols = residual.shape
    half = rows // 2
    feat_size = lax.axis_size("feat")
    tok_size = lax.axis_size("tok")
    assert feat_size == 2 * tok_size and rows % 2 == 0
    my_feat = lax.axis_index("feat")
    core = my_feat & 1
    pieces = gather_half(residual)
    other_weight = exchange(enc_weight, "feat", 1)
    other_gate = exchange(jnp.stack([enc_bias, threshold]), "feat", 1)
    other_probe = exchange(probe_weight, "feat", 1)
    full_width = cols * feat_size
    square_sum = None
    for _, piece in pieces:
        values = piece.astype(jnp.float32)
        part = jnp.sum(values * values, axis=1)
        square_sum = part if square_sum is None else square_sum + part
    scale = lax.rsqrt(square_sum / full_width + epsilon)[:, None]
    whole = jnp.zeros((pieces[0][1].shape[0], full_width), residual.dtype)
    for chip, piece in pieces:
        whole = lax.dynamic_update_slice(whole, piece, (0, chip * 2 * cols))
    normed = (whole.astype(jnp.float32) * scale).astype(jnp.bfloat16)
    preact = [
        jnp.dot(normed, weight, preferred_element_type=jnp.float32)
        for weight in (enc_weight, other_weight)
    ]
    gates = ((enc_bias, threshold), (other_gate[0], other_gate[1]))
    features = []
    for g in range(2):
        encode_preact = preact[g] + gates[g][0]
        gate = jax.nn.sigmoid((encode_preact - gates[g][1]) / smooth_width)
        features.append((encode_preact * gate).astype(jnp.bfloat16))
    partial_value = jnp.dot(features[0], probe_weight, preferred_element_type=jnp.float32)
    partial_value = partial_value + jnp.dot(features[1], other_probe, preferred_element_type=jnp.float32)
    logits = reduce_sum(partial_value)
    classes = probe_weight.shape[1]
    class_ids = jnp.arange(classes, dtype=jnp.int32)
    bits = tok_bits_of()
    block_order = [reverse_bits(p, bits) for p in range(tok_size)]
    label_rows = labels.reshape(tok_size, rows)[jnp.array(block_order, jnp.int32)]
    my_labels = lax.dynamic_slice_in_dim(label_rows, core * half, half, 1).reshape(-1)
    softmax_logits = logits + probe_bias
    exps = jnp.exp(softmax_logits)
    totals = jnp.sum(exps, axis=1, keepdims=True)
    onehot = (my_labels[:, None] == class_ids[None, :]).astype(jnp.float32)
    losses = jnp.log(totals[:, 0]) - jnp.sum(onehot * softmax_logits, axis=1)
    delta = (exps / totals - onehot).astype(jnp.bfloat16)
    num_tokens = tok_size * rows
    share_rows = num_tokens // (feat_size * tok_size)
    start = lax.axis_index(("feat", "tok")) * share_rows
    token_loss = lax.dynamic_slice_in_dim(
        losses, reverse_bits(start // rows, bits) * half + start % rows - core * half, share_rows, 0
    )
    gradient = jnp.dot(features[0].T, delta, preferred_element_type=jnp.float32)
    gradient_other = jnp.dot(features[1].T, delta, preferred_element_type=jnp.float32)
    gradient = gradient + exchange(gradient_other, "feat", 1)
    return (gradient, token_loss)


def solution(mesh):
    in_specs = (
        P("tok", "feat"),
        P(None, ("feat", "tok")),
        P(("feat", "tok")),
        P(("feat", "tok")),
        P(("feat", "tok"), None),
        P(),
        P(),
    )
    out_specs = (P(("feat", "tok"), None), P(("feat", "tok")))
    return jax.shard_map(local, mesh=mesh, in_specs=in_specs, out_specs=out_specs, check_vma=False)
```

```python
import jax
import jax.numpy as jnp
from jax import lax
from jax.sharding import PartitionSpec as P

epsilon = 1e-06
smooth_width = 0.125


def exchange(value, axis, offset):
    size = lax.axis_size(axis)
    return lax.ppermute(value, axis, [(i, i ^ offset) for i in range(size)])


def tok_partners():
    return list(range(1, lax.axis_size("tok")))


def chip_partners():
    return list(range(2, lax.axis_size("feat"), 2))


def ordered(bit_set, mine, got, axis):
    first = jnp.logical_not(bit_set)
    return jnp.concatenate([jnp.where(first, mine, got), jnp.where(first, got, mine)], axis=axis)


def tok_bits_of():
    return lax.axis_size("tok").bit_length() - 1


def reverse_bits(value, count):
    out = 0 * value
    for i in range(count):
        out = out + (((value >> i) & 1) << (count - 1 - i))
    return out


def gather_half(block):
    rows, cols = block.shape
    half = rows // 2
    my_tok = lax.axis_index("tok")
    my_feat = lax.axis_index("feat")
    core = my_feat & 1
    got = exchange(block, "feat", 1)
    keep = lax.dynamic_slice_in_dim(block, core * half, half, 0)
    theirs = lax.dynamic_slice_in_dim(got, core * half, half, 0)
    held = ordered(core, keep, theirs, 1)
    for bit in reversed(range(tok_bits_of())):
        other = exchange(held, "tok", 1 << bit)
        held = ordered((my_tok >> bit) & 1, held, other, 0)
    my_chip = my_feat >> 1
    pieces = [(my_chip, held)]
    for k in chip_partners():
        pieces.append((my_chip ^ (k >> 1), exchange(held, "feat", k)))
    return pieces


def reduce_sum(value):
    for bit in range(tok_bits_of()):
        value = value + exchange(value, "tok", 1 << bit)
    total = value
    for k in chip_partners():
        total = total + exchange(value, "feat", k)
    return total


def local(residual, enc_weight, enc_bias, threshold, probe_weight, probe_bias, labels):
    rows, cols = residual.shape
    half = rows // 2
    feat_size = lax.axis_size("feat")
    tok_size = lax.axis_size("tok")
    assert feat_size == 2 * tok_size and rows % 2 == 0
    my_feat = lax.axis_index("feat")
    core = my_feat & 1
    pieces = gather_half(residual)
    other_weight = exchange(enc_weight, "feat", 1)
    other_gate = exchange(jnp.stack([enc_bias, threshold]), "feat", 1)
    other_probe = exchange(probe_weight, "feat", 1)
    full_width = cols * feat_size
    square_sum = None
    for _, piece in pieces:
        values = piece.astype(jnp.float32)
        part = jnp.sum(values * values, axis=1)
        square_sum = part if square_sum is None else square_sum + part
    scale = lax.rsqrt(square_sum / full_width + epsilon)[:, None]
    whole = jnp.zeros((pieces[0][1].shape[0], full_width), residual.dtype)
    for chip, piece in pieces:
        whole = lax.dynamic_update_slice(whole, piece, (0, chip * 2 * cols))
    normed = (whole.astype(jnp.float32) * scale).astype(jnp.bfloat16)
    preact = [
        jnp.dot(normed, weight, preferred_element_type=jnp.float32)
        for weight in (enc_weight, other_weight)
    ]
    gates = ((enc_bias, threshold), (other_gate[0], other_gate[1]))
    features = []
    for g in range(2):
        encode_preact = preact[g] + gates[g][0]
        gate = jax.nn.sigmoid((encode_preact - gates[g][1]) / smooth_width)
        features.append((encode_preact * gate).astype(jnp.bfloat16))
    partial_value = jnp.dot(features[0], probe_weight, preferred_element_type=jnp.float32)
    partial_value = partial_value + jnp.dot(features[1], other_probe, preferred_element_type=jnp.float32)
    logits = reduce_sum(partial_value)
    classes = probe_weight.shape[1]
    class_ids = jnp.arange(classes, dtype=jnp.int32)
    bits = tok_bits_of()
    block_order = [reverse_bits(p, bits) for p in range(tok_size)]
    label_rows = labels.reshape(tok_size, rows)[jnp.array(block_order, jnp.int32)]
    my_labels = lax.dynamic_slice_in_dim(label_rows, core * half, half, 1).reshape(-1)
    softmax_logits = logits + probe_bias
    exps = jnp.exp(softmax_logits)
    totals = jnp.sum(exps, axis=1, keepdims=True)
    onehot = (my_labels[:, None] == class_ids[None, :]).astype(jnp.float32)
    losses = jnp.log(totals[:, 0]) - jnp.sum(onehot * softmax_logits, axis=1)
    delta = (exps / totals - onehot).astype(jnp.bfloat16)
    num_tokens = tok_size * rows
    share_rows = num_tokens // (feat_size * tok_size)
    start = lax.axis_index(("feat", "tok")) * share_rows
    token_loss = lax.dynamic_slice_in_dim(
        losses, reverse_bits(start // rows, bits) * half + start % rows - core * half, share_rows, 0
    )
    gradient = jnp.dot(features[0].T, delta, preferred_element_type=jnp.float32)
    gradient_other = jnp.dot(features[1].T, delta, preferred_element_type=jnp.float32)
    gradient = gradient + exchange(gradient_other, "feat", 1)
    return (gradient, token_loss)


def solution(mesh):
    in_specs = (
        P("tok", "feat"),
        P(None, ("feat", "tok")),
        P(("feat", "tok")),
        P(("feat", "tok")),
        P(("feat", "tok"), None),
        P(),
        P(),
    )
    out_specs = (P(("feat", "tok"), None), P(("feat", "tok")))
    return jax.shard_map(local, mesh=mesh, in_specs=in_specs, out_specs=out_specs, check_vma=False)
```
